128 devices in a mesh: seq: 32 (over z, x, y_lo), type: 4 (over y_hi, core).
Axes of the slice: x: 4, y: 4 (y_hi: 2, y_lo: 2; y = y_hi * 2 + y_lo), z: 4, core: 2. Of those that a mesh axis runs over, the one named last changes fastest.
Arguments:
- tokens: bfloat16 [17408, 1024], P(('seq', 'type')), may hold values from -60 to 60
- shift_scale: float32 [2, 1024], replicated, may hold values from -0.8 to 0.8
- branch_gate: float32 [1024], replicated, may hold values from 0.25 to 1.75
- final_gain: float32 [1024], replicated, may hold values from 0.5 to 1.5
- w_qkv: bfloat16 [3, 1024, 1024], P(None, None, 'type'), may hold values from -1 to 1
- w_out: bfloat16 [1024, 1024], P('type'), may hold values from -0.375 to 0.375
- type_ids: int32 [17408, 1], P(('seq', 'type')), may hold values from 0 to 7; in each aligned block of 136 rows (0 to 135, 136 to 271, ...) at most 51 rows name the same one
- head_w1: bfloat16 [8, 1024, 1024], P('type'), may hold values from -0.1875 to 0.1875
- head_b1: bfloat16 [8, 1024], P('type'), may hold values from -3 to 3
- head_w2: bfloat16 [8, 1024, 16], P('type'), may hold values from -0.1875 to 0.1875
Outputs:
- updated: bfloat16 [17408, 1024], P(('seq', 'type'))
- head_out: float32 [17408, 16], P(('seq', 'type'))
The draws below stay inside these ranges and needn't reach their ends.
Inputs may be any that keep to these rules, and one draw needn't show every extreme that they name: `type_ids`: among the 136 tokens of one device no type occurs more than 51 times; some type occurs exactly 51 times on some devices.
All inputs are finite; a program needn't handle non-finite values.
Results may differ from the reference program's by a relative error of at most 0.014.
Values may be sent and summed in bfloat16 or wider, within the bound.
No kernel may reach another device: no remote copies, remote signals or barrier semaphores. Data moves between devices by JAX's collectives and lax.ppermute only.
A program may use at most 192 MiB of HBM per device.

```python
import math
import jax
import jax.numpy as jnp
import numpy as np
from jax import lax

D = 1024
HEADS = 16
HD = 64
HH = 1024
OUTS = 16
TOK_DEV = 136
TOKENS = 17408
NTYPES = 8
CAP = 51


def draw_tokens(key, part):
    groups = TOKENS // 8
    members = jax.random.randint(jax.random.fold_in(key, 6), (TOKENS,), 0, groups)
    row_scales = jnp.exp(jax.random.uniform(jax.random.fold_in(key, 1), (TOKENS, 1), jnp.float32, jnp.log(0.3), jnp.log(3.0)))
    col_scales = jnp.exp(jax.random.uniform(jax.random.fold_in(key, 2), (1, D), jnp.float32, jnp.log(0.3), jnp.log(3.0)))
    centers = jax.random.normal(jax.random.fold_in(key, 3), (groups, D), jnp.float32)
    jitter = jax.random.normal(jax.random.fold_in(key, 4), (TOKENS, D), jnp.float32)
    blended = 0.95 * centers[members] + 0.32 * jitter
    values = blended * row_scales * col_scales
    values = 0.25 * values
    return jnp.clip(values, -60.0, 60.0).astype(jnp.bfloat16)


def draw_w_qkv(key, part):
    query_spread = 2.0 / D ** 0.5
    value_spread = 1.0 / D ** 0.5
    basis = jax.random.normal(jax.random.fold_in(key, 5), (3, D, HEADS * HD), jnp.float32)
    basis = jnp.clip(basis, -6.0, 6.0)
    query_part = basis[0] * query_spread
    key_part = (0.4 * basis[0] + 0.5 * basis[1]) * query_spread
    value_part = basis[2] * value_spread
    values = jnp.stack([query_part, key_part, value_part], axis=0)
    return jnp.clip(values, -1.0, 1.0).astype(jnp.bfloat16)


def block_scale(key, dims, cuts, smallest, high):
    loudness, own = 1.0, jax.random.fold_in(key, 6)
    for dim, shards_of in cuts:
        steps = jnp.exp(jax.random.uniform(jax.random.fold_in(own, dim), (shards_of,), jnp.float32, smallest / len(cuts), high / len(cuts)))
        loudness = loudness * jnp.repeat(steps, dims[dim] // shards_of).reshape([-1 if axis == dim else 1 for axis in range(len(dims))])
    return loudness


def shared_out(key, own, number, rows, number_of, top, bound, slope):
    sequence = jax.random.permutation(key, number_of)
    packed, ordinary = shares(number_of, rows * top, bound, slope, True), shares(number_of, rows * top, bound, slope, False)
    places = jnp.arange(number_of)

    def named(tallies, rotation):
        used = int((tallies > 0).sum())
        fixed = max(1, used // 4)
        shifted = fixed + (places - fixed + rotation * (used - fixed)) % max(1, number_of - fixed)
        return jnp.zeros((number_of,), jnp.int32).at[sequence[jnp.where(places < fixed, places, shifted)]].set(jnp.asarray(tallies, jnp.int32))

    tallies = jnp.where(number % 4 == 0, named(packed, number // 4), named(ordinary, number - number // 4 - 1))
    mixed = jax.random.permutation(jax.random.fold_in(own, 3), number_of)
    source_of, taker = mixed[0:number_of // 2 * 2:2], mixed[1:number_of // 2 * 2:2]
    room = jnp.minimum(tallies[source_of] - 1, bound - tallies[taker]) // 2
    room = jnp.where((source_of == sequence[0]) | (taker == sequence[0]) | (tallies[taker] == 0), 0, jnp.maximum(room, 0))
    shifted = jax.random.randint(jax.random.fold_in(own, 4), (number_of // 2,), 0, 1 << 20) % (room + 1)
    tallies = tallies.at[source_of].add(-shifted).at[taker].add(shifted)
    items = jnp.searchsorted(jnp.cumsum(tallies), jnp.arange(rows * top), side="right").astype(jnp.int32)
    listing = items.reshape(top, rows).T
    listing = listing[jax.random.permutation(jax.random.fold_in(own, 1), rows)]
    rotation = jax.random.randint(jax.random.fold_in(own, 2), (rows, 1), 0, top)
    return jnp.take_along_axis(listing, (jnp.arange(top)[None, :] + rotation) % top, axis=1)


def shares(number_of, total, reach, lean, full):
    loads = [(1 << 20) // math.isqrt(rank ** lean) + 1 for rank in range(1, number_of + 1)]
    largest = reach if full else min(reach, max(-(-total // number_of), total * loads[0] // sum(loads)))
    least = 1 if total - largest >= number_of - 1 else 0
    given, surplus = [largest] + [least] * (number_of - 1), total - largest - least * (number_of - 1)
    while surplus > 0:
        free = [i for i in range(1, number_of) if given[i] < largest] or [i for i in range(1, number_of) if given[i] < reach]
        pool, remaining = sum([loads[i] for i in free]), surplus
        for i in free:
            addition = min(reach - given[i], max(1, remaining * loads[i] // pool), surplus)
            given[i] = given[i] + addition
            surplus = surplus - addition
    return np.array(given)


def gaussian(rng, shape, width, reach, cuts=(), held_as=jnp.bfloat16):
    entries = width * jax.random.normal(rng, shape, jnp.float32)
    if cuts:
        entries = entries * block_scale(rng, shape, cuts, -0.22, 0.18)
    return jnp.clip(entries, -reach, reach).astype(held_as)


def setup_inputs(seed: int = 0) -> dict:
    keys = jax.random.split(jax.random.key(seed), 11)
    tokens = draw_tokens(jax.random.fold_in(keys[10], 71), 0)
    shift_scale = gaussian(keys[1], (2, D), 0.2, 0.8, (), jnp.float32)
    branch_gate = jnp.clip(1.0 + 0.15 * jax.random.normal(keys[2], (D,), jnp.float32), 0.25, 1.75)
    final_gain = jnp.clip(1.0 + 0.1 * jax.random.normal(keys[3], (D,), jnp.float32), 0.5, 1.5)
    w_qkv = draw_w_qkv(jax.random.fold_in(keys[10], 71), 0)
    w_out = gaussian(keys[5], (HEADS * HD, D), (HEADS * HD // 4) ** -0.5, 0.375, ((0, 4),))
    type_ids_keys = jax.random.split(jax.random.fold_in(keys[6], 1), TOKENS // TOK_DEV)
    type_ids_turns = jax.random.permutation(jax.random.fold_in(keys[6], 3), TOKENS // TOK_DEV)
    type_ids = jax.vmap(lambda own, number: shared_out(jax.random.fold_in(keys[6], 2), own, number, TOK_DEV, NTYPES, 1, CAP, 2))(type_ids_keys, type_ids_turns).reshape((TOKENS, 1))
    head_w1 = gaussian(keys[7], (NTYPES, D, HH), D ** -0.5, 0.1875, ((0, 4),))
    head_b1 = gaussian(keys[8], (NTYPES, HH), 0.5, 3.0, ((0, 4),))
    head_w2 = gaussian(keys[9], (NTYPES, HH, OUTS), HH ** -0.5, 0.1875, ((0, 4),))
    return {"tokens": tokens, "shift_scale": shift_scale, "branch_gate": branch_gate, "final_gain": final_gain, "w_qkv": w_qkv, "w_out": w_out, "type_ids": type_ids, "head_w1": head_w1, "head_b1": head_b1, "head_w2": head_w2}


def rms_normalize(values):
    squares = lax.optimization_barrier(jnp.mean(values * values, axis=-1, keepdims=True))
    return values * lax.rsqrt(squares + 1e-06)

def reference(tokens, shift_scale, branch_gate, final_gain, w_qkv, w_out, type_ids, head_w1, head_b1, head_w2):
    inputs = tokens.astype(jnp.float32)
    modulated = (rms_normalize(inputs) * (1.0 + shift_scale[1]) + shift_scale[0]).astype(jnp.bfloat16)
    projected = [jnp.dot(modulated.astype(jnp.float32), w_qkv[which].astype(jnp.float32), preferred_element_type=jnp.float32).astype(jnp.bfloat16) for which in range(3)]
    queries = projected[0].astype(jnp.float32).reshape(TOKENS, HEADS, HD)
    all_keys = projected[1].astype(jnp.float32).reshape(TOKENS, HEADS, HD)
    all_values = projected[2].astype(jnp.float32).reshape(TOKENS, HEADS, HD)
    factor = HD ** (-0.5)

    def attend(query_block):
        scores = jnp.einsum('qhd,khd->hqk', query_block, all_keys) * factor
        largest = lax.optimization_barrier(jnp.max(scores, axis=-1, keepdims=True))
        weights = jnp.exp(scores - largest)
        totals = lax.optimization_barrier(jnp.sum(weights, axis=-1))
        rounded = lax.optimization_barrier(weights.astype(jnp.bfloat16)).astype(jnp.float32)
        numer = jnp.einsum('hqk,khd->qhd', rounded, all_values)
        return (numer / jnp.transpose(totals)[:, :, None]).astype(jnp.bfloat16)
    block_rows = min(256, TOKENS)
    attended = lax.map(attend, queries.reshape(TOKENS // block_rows, block_rows, HEADS, HD))
    attended = attended.reshape(TOKENS, HEADS * HD)
    mixed = jnp.dot(attended.astype(jnp.float32), w_out.astype(jnp.float32), preferred_element_type=jnp.float32)
    updated = (inputs + branch_gate * mixed).astype(jnp.bfloat16)
    final = (rms_normalize(updated.astype(jnp.float32)) * final_gain).astype(jnp.bfloat16)
    kinds = type_ids[:, 0]
    head_out = jnp.zeros((TOKENS, OUTS), jnp.float32)
    for kind in range(NTYPES):
        hidden = jax.nn.gelu(jnp.dot(final.astype(jnp.float32), head_w1[kind].astype(jnp.float32), preferred_element_type=jnp.float32) + head_b1[kind].astype(jnp.float32)).astype(jnp.bfloat16)
        result = jnp.dot(hidden.astype(jnp.float32), head_w2[kind].astype(jnp.float32), preferred_element_type=jnp.float32)
        head_out = jnp.where((kinds == kind)[:, None], result, head_out)
    return (updated, head_out)
```

```python
import jax
import jax.numpy as jnp
from jax import lax
from jax.experimental import pallas as pl
from jax.experimental.pallas import tpu as pltpu
from jax.sharding import Mesh
from jax.sharding import PartitionSpec as P

HD = 64
SCALE = HD ** (-0.5)
SUB = 4
QUERY_BLOCK = 544


def rms_normalize(values):
    squares = jnp.mean(values * values, axis=-1, keepdims=True)
    return values * lax.rsqrt(squares + 1e-06)


def flash_kernel(q_ref, kv_ref, o_ref, m_ref, l_ref, acc_ref):
    step = pl.program_id(1)

    @pl.when(step == 0)
    def _():
        m_ref[...] = jnp.full(m_ref.shape, -jnp.inf, jnp.float32)
        l_ref[...] = jnp.zeros(l_ref.shape, jnp.float32)
        acc_ref[...] = jnp.zeros(acc_ref.shape, jnp.float32)

    q = q_ref[...]
    kv = kv_ref[...]
    scores = lax.dot_general(q, kv, (((1,), (1,)), ((), ())), preferred_element_type=jnp.float32)
    m_old = m_ref[...]
    m_new = jnp.maximum(m_old, jnp.max(scores, axis=1, keepdims=True))
    decay = jnp.exp((m_old - m_new) * SCALE)
    weights = jnp.exp((scores - m_new) * SCALE)
    l_ref[...] = decay * l_ref[...] + jnp.sum(weights, axis=1, keepdims=True)
    acc_ref[...] = decay * acc_ref[...] + jnp.dot(
        weights.astype(jnp.bfloat16), kv, preferred_element_type=jnp.float32
    )
    m_ref[...] = m_new

    @pl.when(step == pl.num_programs(1) - 1)
    def _():
        o_ref[...] = (acc_ref[...] / l_ref[...]).astype(o_ref.dtype)


def flash(q_pad, kv_all):
    rows, width = q_pad.shape
    chunks, chunk, _ = kv_all.shape
    block = QUERY_BLOCK
    return pl.pallas_call(
        flash_kernel,
        grid=(rows // block, chunks),
        in_specs=[
            pl.BlockSpec((block, width), lambda i, k: (i, 0)),
            pl.BlockSpec((None, chunk, width), lambda i, k: (k, 0, 0)),
        ],
        out_specs=pl.BlockSpec((block, width), lambda i, k: (i, 0)),
        out_shape=jax.ShapeDtypeStruct((rows, width), jnp.bfloat16),
        scratch_shapes=[
            pltpu.VMEM((block, 1), jnp.float32),
            pltpu.VMEM((block, 1), jnp.float32),
            pltpu.VMEM((block, width), jnp.float32),
        ],
        compiler_params=pltpu.CompilerParams(dimension_semantics=("parallel", "arbitrary")),
        cost_estimate=pl.CostEstimate(
            flops=4 * rows * chunks * chunk * width,
            transcendentals=rows * chunks * chunk,
            bytes_accessed=2 * (rows * width * 2 + (rows // block) * chunks * chunk * width),
        ),
    )(q_pad, kv_all)


def body(
    tokens, shift_scale, branch_gate, final_gain, w_qkv, w_out, type_ids, head_w1, head_b1, head_w2
):
    inputs = tokens.astype(jnp.float32)
    modulated = (rms_normalize(inputs) * (1.0 + shift_scale[1]) + shift_scale[0]).astype(
        jnp.bfloat16
    )
    gathered = lax.all_gather(modulated, "type", axis=0, tiled=True)
    dim = w_qkv.shape[1]
    local_heads = w_qkv.shape[2] // HD
    parts = w_qkv.reshape(3, dim, local_heads, HD)
    arranged = jnp.stack([parts[0], jnp.zeros_like(parts[0]), parts[1], parts[2]], axis=2)
    arranged = arranged.reshape(dim, local_heads, 4 * HD)
    projected = jnp.einsum(
        "rd,dje->jre", gathered, arranged, preferred_element_type=jnp.float32
    ).astype(jnp.bfloat16)
    mine = lax.all_to_all(projected, "sub", 0, 0, tiled=True)
    mine = mine.reshape(-1, 4 * HD)
    q_pad = mine[:, : 2 * HD]
    kv_local = mine[:, 2 * HD :]
    kv_all = lax.all_gather(kv_local, "grp", axis=0, tiled=False)
    attended = flash(q_pad, kv_all)[:, HD:]
    attended = attended.reshape(local_heads, -1, HD)
    back = lax.all_to_all(attended, "sub", 0, 0, tiled=True)
    rows = back.shape[1]
    back = jnp.transpose(back, (1, 0, 2)).reshape(rows, local_heads * HD)
    mixed = lax.psum_scatter(
        jnp.dot(back, w_out, preferred_element_type=jnp.float32),
        "type",
        scatter_dimension=0,
        tiled=True,
    )
    updated = (inputs + branch_gate * mixed).astype(jnp.bfloat16)
    final = (rms_normalize(updated.astype(jnp.float32)) * final_gain).astype(jnp.bfloat16)
    final_all = lax.all_gather(final, "type", axis=0, tiled=True)
    kinds_all = lax.all_gather(type_ids[:, 0], "type", axis=0, tiled=True)
    owned = head_w1.shape[0]
    first_kind = lax.axis_index("type") * owned
    result = jnp.zeros((final_all.shape[0], head_w2.shape[2]), jnp.float32)
    for which in range(owned):
        hidden = jnp.dot(final_all, head_w1[which], preferred_element_type=jnp.float32)
        hidden = jax.nn.gelu(hidden + head_b1[which].astype(jnp.float32)).astype(jnp.bfloat16)
        answer = jnp.dot(hidden, head_w2[which], preferred_element_type=jnp.float32)
        result = jnp.where((kinds_all == first_kind + which)[:, None], answer, result)
    head_out = lax.psum_scatter(result, "type", scatter_dimension=0, tiled=True)
    return (updated, head_out)


def solution(mesh):
    seq = mesh.shape["seq"]
    kinds = mesh.shape["type"]
    split = Mesh(mesh.devices.reshape(seq // SUB, SUB, kinds), ("grp", "sub", "type"))
    rows = P(("grp", "sub", "type"), None)
    in_specs = (
        rows,
        P(),
        P(),
        P(),
        P(None, None, "type"),
        P("type", None),
        rows,
        P("type", None, None),
        P("type", None),
        P("type", None, None),
    )
    out_specs = (rows, rows)
    return jax.shard_map(body, mesh=split, in_specs=in_specs, out_specs=out_specs, check_vma=False)
```

```python
import functools

import jax
import jax.numpy as jnp
from jax import lax
from jax.experimental import pallas as pl
from jax.experimental.pallas import tpu as pltpu
from jax.sharding import Mesh
from jax.sharding import PartitionSpec as P

HD = 64
SCALE = HD ** (-0.5)
QUERY_BLOCK = 544
KEY_BLOCK = 544
RING = ("z", "y")


def rms_normalize(values):
    squares = jnp.mean(values * values, axis=-1, keepdims=True)
    return values * lax.rsqrt(squares + 1e-06)


def step_kernel(first, last, *refs):
    if first:
        q_ref, kv_ref = refs[:2]
        rest = refs[2:]
    else:
        q_ref, kv_ref, m_in, l_in, acc_in = refs[:5]
        rest = refs[5:]
    m_s, l_s, acc_s = rest[-3:]
    outs = rest[:-3]
    if first:
        m_s[...] = jnp.full(m_s.shape, -jnp.inf, jnp.float32)
        l_s[...] = jnp.zeros(l_s.shape, jnp.float32)
        acc_s[...] = jnp.zeros(acc_s.shape, jnp.float32)
    else:
        m_s[...] = m_in[...]
        l_s[...] = l_in[...]
        acc_s[...] = acc_in[...]
    q = q_ref[...]

    def absorb(c, carry):
        start = pl.multiple_of(c * KEY_BLOCK, KEY_BLOCK)
        kv = kv_ref[pl.ds(start, KEY_BLOCK), :]
        scores = lax.dot_general(
            q, kv, (((1,), (1,)), ((), ())), preferred_element_type=jnp.float32
        )
        m_old = m_s[...]
        m_new = jnp.maximum(m_old, jnp.max(scores, axis=1, keepdims=True))
        decay = jnp.exp((m_old - m_new) * SCALE)
        weights = jnp.exp((scores - m_new) * SCALE)
        l_s[...] = decay * l_s[...] + jnp.sum(weights, axis=1, keepdims=True)
        acc_s[...] = decay * acc_s[...] + jnp.dot(
            weights.astype(jnp.bfloat16), kv, preferred_element_type=jnp.float32
        )
        m_s[...] = m_new
        return carry

    lax.fori_loop(0, kv_ref.shape[0] // KEY_BLOCK, absorb, 0)
    if last:
        outs[0][...] = (acc_s[...] / l_s[...]).astype(outs[0].dtype)
    else:
        outs[0][...] = m_s[...]
        outs[1][...] = l_s[...]
        outs[2][...] = acc_s[...]


def flash_step(q_pad, kv, state, first, last):
    rows, width = q_pad.shape
    chunk = kv.shape[0]
    block = QUERY_BLOCK
    row_block = pl.BlockSpec((block, width), lambda i: (i, 0))
    stat_block = pl.BlockSpec((block, 1), lambda i: (i, 0))
    in_specs = [row_block, pl.BlockSpec((chunk, width), lambda i: (0, 0))]
    operands = [q_pad, kv]
    if not first:
        in_specs += [stat_block, stat_block, row_block]
        operands += list(state)
    if last:
        out_specs = row_block
        out_shape = jax.ShapeDtypeStruct((rows, width), jnp.bfloat16)
    else:
        out_specs = [stat_block, stat_block, row_block]
        out_shape = [
            jax.ShapeDtypeStruct((rows, 1), jnp.float32),
            jax.ShapeDtypeStruct((rows, 1), jnp.float32),
            jax.ShapeDtypeStruct((rows, width), jnp.float32),
        ]
    return pl.pallas_call(
        functools.partial(step_kernel, first, last),
        grid=(rows // block,),
        in_specs=in_specs,
        out_specs=out_specs,
        out_shape=out_shape,
        scratch_shapes=[
            pltpu.VMEM((block, 1), jnp.float32),
            pltpu.VMEM((block, 1), jnp.float32),
            pltpu.VMEM((block, width), jnp.float32),
        ],
        compiler_params=pltpu.CompilerParams(dimension_semantics=("arbitrary",)),
        cost_estimate=pl.CostEstimate(
            flops=4 * rows * chunk * width,
            transcendentals=rows * chunk,
            bytes_accessed=rows * width * 14 + chunk * width * 2,
        ),
    )(*operands)


def body(
    tokens, shift_scale, branch_gate, final_gain, w_qkv, w_out, type_ids, head_w1, head_b1, head_w2
):
    inputs = tokens.astype(jnp.float32)
    modulated = (rms_normalize(inputs) * (1.0 + shift_scale[1]) + shift_scale[0]).astype(
        jnp.bfloat16
    )
    gathered = lax.all_gather(modulated, "type", axis=0, tiled=True)
    dim = w_qkv.shape[1]
    local_heads = w_qkv.shape[2] // HD
    kinds = lax.axis_size("type")
    parts = w_qkv.reshape(3, dim, local_heads, HD)
    arranged = jnp.stack([parts[0], jnp.zeros_like(parts[0]), parts[1], parts[2]], axis=2)
    arranged = arranged.reshape(dim, local_heads, 4 * HD)
    projected = jnp.einsum(
        "rd,dje->jre", gathered, arranged, preferred_element_type=jnp.float32
    ).astype(jnp.bfloat16)
    mine = lax.all_to_all(projected, "x", 0, 0, tiled=True)
    mine = mine.reshape(-1, 4 * HD)
    q_pad = mine[:, : 2 * HD]
    chunk = mine[:, 2 * HD :]
    w_out_dep, chunk = lax.optimization_barrier((w_out, chunk))
    w_out_all = lax.all_gather(w_out_dep, "type", axis=0, tiled=True)
    z_n = lax.axis_size("z")
    y_n = lax.axis_size("y")
    order = [z * y_n for z in range(z_n)] + [z * y_n + 1 for z in reversed(range(z_n))]
    if y_n != 2:
        order = list(range(z_n * y_n))
    pairs = [(order[i], order[(i + 1) % len(order)]) for i in range(len(order))]
    steps = len(order)
    state = None
    for step in range(steps):
        if step < steps - 1:
            coming = lax.ppermute(chunk, RING, pairs)
        state = flash_step(q_pad, chunk, state, step == 0, step == steps - 1)
        if step < steps - 1:
            chunk, state = lax.optimization_barrier((coming, state))
    attended = state[:, HD:]
    rows = tokens.shape[0]
    attended = attended.reshape(-1, kinds, rows, HD).reshape(-1, rows, HD)
    back = lax.all_to_all(attended, ("x", "type"), 0, 0, tiled=True)
    back = back.reshape(-1, kinds, rows, HD)
    back = jnp.transpose(back, (2, 1, 0, 3)).reshape(rows, -1)
    mixed = jnp.dot(back, w_out_all, preferred_element_type=jnp.float32)
    updated = (inputs + branch_gate * mixed).astype(jnp.bfloat16)
    final = (rms_normalize(updated.astype(jnp.float32)) * final_gain).astype(jnp.bfloat16)
    final_all = lax.all_gather(final, "type", axis=0, tiled=True)
    kinds_all = lax.all_gather(type_ids[:, 0], "type", axis=0, tiled=True)
    owned = head_w1.shape[0]
    first_kind = lax.axis_index("type") * owned
    result = jnp.zeros((final_all.shape[0], head_w2.shape[2]), jnp.float32)
    for which in range(owned):
        hidden = jnp.dot(final_all, head_w1[which], preferred_element_type=jnp.float32)
        hidden = jax.nn.gelu(hidden + head_b1[which].astype(jnp.float32)).astype(jnp.bfloat16)
        answer = jnp.dot(hidden, head_w2[which], preferred_element_type=jnp.float32)
        result = jnp.where((kinds_all == first_kind + which)[:, None], answer, result)
    head_out = lax.psum_scatter(result, "type", scatter_dimension=0, tiled=True)
    return (updated, head_out)


def solution(mesh):
    seq = mesh.shape["seq"]
    kinds = mesh.shape["type"]
    y_n = 2
    x_n = 4
    z_n = seq // (x_n * y_n)
    split = Mesh(mesh.devices.reshape(z_n, x_n, y_n, kinds), ("z", "x", "y", "type"))
    rows = P(("z", "x", "y", "type"), None)
    in_specs = (
        rows,
        P(),
        P(),
        P(),
        P(None, None, "type"),
        P("type", None),
        rows,
        P("type", None, None),
        P("type", None),
        P("type", None, None),
    )
    out_specs = (rows, rows)
    return jax.shard_map(body, mesh=split, in_specs=in_specs, out_specs=out_specs, check_vma=False)
```

```python
import functools

import jax
import jax.numpy as jnp
from jax import lax
from jax.experimental import pallas as pl
from jax.experimental.pallas import tpu as pltpu
from jax.sharding import Mesh
from jax.sharding import PartitionSpec as P

HD = 64
SCALE = HD ** (-0.5)
QUERY_BLOCK = 272
KEY_BLOCK = 2176
RING = ("z", "y")


def rms_normalize(values):
    squares = jnp.mean(values * values, axis=-1, keepdims=True)
    return values * lax.rsqrt(squares + 1e-06)


def step_kernel(first, last, *refs):
    if first:
        q_ref, kv_ref = refs[:2]
        rest = refs[2:]
    else:
        q_ref, kv_ref, m_in, l_in, acc_in = refs[:5]
        rest = refs[5:]
    m_s, l_s, acc_s = rest[-3:]
    outs = rest[:-3]
    if first:
        m_s[...] = jnp.full(m_s.shape, -jnp.inf, jnp.float32)
        l_s[...] = jnp.zeros(l_s.shape, jnp.float32)
        acc_s[...] = jnp.zeros(acc_s.shape, jnp.float32)
    else:
        m_s[...] = m_in[...]
        l_s[...] = l_in[...]
        acc_s[...] = acc_in[...]
    q = q_ref[...]

    def absorb(c, carry):
        start = pl.multiple_of(c * KEY_BLOCK, KEY_BLOCK)
        kv = kv_ref[pl.ds(start, KEY_BLOCK), :]
        scores = lax.dot_general(
            q, kv, (((1,), (1,)), ((), ())), preferred_element_type=jnp.float32
        )
        m_old = m_s[...]
        m_new = jnp.maximum(m_old, jnp.max(scores, axis=1, keepdims=True))
        decay = jnp.exp((m_old - m_new) * SCALE)
        weights = jnp.exp((scores - m_new) * SCALE)
        l_s[...] = decay * l_s[...] + jnp.sum(weights, axis=1, keepdims=True)
        acc_s[...] = decay * acc_s[...] + jnp.dot(
            weights.astype(jnp.bfloat16), kv, preferred_element_type=jnp.float32
        )
        m_s[...] = m_new
        return carry

    lax.fori_loop(0, kv_ref.shape[0] // KEY_BLOCK, absorb, 0)
    if last:
        outs[0][...] = (acc_s[...] / l_s[...]).astype(outs[0].dtype)
    else:
        outs[0][...] = m_s[...]
        outs[1][...] = l_s[...]
        outs[2][...] = acc_s[...]


def flash_step(q_pad, kv, state, first, last):
    rows, width = q_pad.shape
    chunk = kv.shape[0]
    block = QUERY_BLOCK
    row_block = pl.BlockSpec((block, width), lambda i: (i, 0))
    stat_block = pl.BlockSpec((block, 1), lambda i: (i, 0))
    in_specs = [row_block, pl.BlockSpec((chunk, width), lambda i: (0, 0))]
    operands = [q_pad, kv]
    if not first:
        in_specs += [stat_block, stat_block, row_block]
        operands += list(state)
    if last:
        out_specs = row_block
        out_shape = jax.ShapeDtypeStruct((rows, width), jnp.bfloat16)
    else:
        out_specs = [stat_block, stat_block, row_block]
        out_shape = [
            jax.ShapeDtypeStruct((rows, 1), jnp.float32),
            jax.ShapeDtypeStruct((rows, 1), jnp.float32),
            jax.ShapeDtypeStruct((rows, width), jnp.float32),
        ]
    return pl.pallas_call(
        functools.partial(step_kernel, first, last),
        grid=(rows // block,),
        in_specs=in_specs,
        out_specs=out_specs,
        out_shape=out_shape,
        scratch_shapes=[
            pltpu.VMEM((block, 1), jnp.float32),
            pltpu.VMEM((block, 1), jnp.float32),
            pltpu.VMEM((block, width), jnp.float32),
        ],
        compiler_params=pltpu.CompilerParams(dimension_semantics=("arbitrary",)),
        cost_estimate=pl.CostEstimate(
            flops=4 * rows * chunk * width,
            transcendentals=rows * chunk,
            bytes_accessed=rows * width * 14 + chunk * width * 2,
        ),
    )(*operands)


def body(
    tokens, shift_scale, branch_gate, final_gain, w_qkv, w_out, type_ids, head_w1, head_b1, head_w2
):
    inputs = tokens.astype(jnp.float32)
    modulated = (rms_normalize(inputs) * (1.0 + shift_scale[1]) + shift_scale[0]).astype(
        jnp.bfloat16
    )
    gathered = lax.all_gather(modulated, "type", axis=0, tiled=True)
    dim = w_qkv.shape[1]
    local_heads = w_qkv.shape[2] // HD
    kinds = lax.axis_size("type")
    parts = w_qkv.reshape(3, dim, local_heads, HD)
    arranged = jnp.stack([parts[0], jnp.zeros_like(parts[0]), parts[1], parts[2]], axis=2)
    arranged = arranged.reshape(dim, local_heads, 4 * HD)
    projected = jnp.einsum(
        "rd,dje->jre", gathered, arranged, preferred_element_type=jnp.float32
    ).astype(jnp.bfloat16)
    mine = lax.all_to_all(projected, "x", 0, 0, tiled=True)
    mine = mine.reshape(-1, 4 * HD)
    q_pad = mine[:, : 2 * HD]
    chunk = mine[:, 2 * HD :]
    w_out_dep, chunk = lax.optimization_barrier((w_out, chunk))
    w_out_all = lax.all_gather(w_out_dep, "type", axis=0, tiled=True)
    z_n = lax.axis_size("z")
    y_n = lax.axis_size("y")
    order = [z * y_n for z in range(z_n)] + [z * y_n + 1 for z in reversed(range(z_n))]
    if y_n != 2:
        order = list(range(z_n * y_n))
    pairs = [(order[i], order[(i + 1) % len(order)]) for i in range(len(order))]
    steps = len(order)
    state = None
    for step in range(steps):
        if step < steps - 1:
            coming = lax.ppermute(chunk, RING, pairs)
        state = flash_step(q_pad, chunk, state, step == 0, step == steps - 1)
        if step < steps - 1:
            chunk, state = lax.optimization_barrier((coming, state))
    attended = state[:, HD:]
    rows = tokens.shape[0]
    attended = attended.reshape(-1, kinds, rows, HD).reshape(-1, rows, HD)
    back = lax.all_to_all(attended, ("x", "type"), 0, 0, tiled=True)
    back = back.reshape(-1, kinds, rows, HD)
    back = jnp.transpose(back, (2, 1, 0, 3)).reshape(rows, -1)
    mixed = jnp.dot(back, w_out_all, preferred_element_type=jnp.float32)
    updated = (inputs + branch_gate * mixed).astype(jnp.bfloat16)
    final = (rms_normalize(updated.astype(jnp.float32)) * final_gain).astype(jnp.bfloat16)
    final_all = lax.all_gather(final, "type", axis=0, tiled=True)
    kinds_all = lax.all_gather(type_ids[:, 0], "type", axis=0, tiled=True)
    owned = head_w1.shape[0]
    first_kind = lax.axis_index("type") * owned
    result = jnp.zeros((final_all.shape[0], head_w2.shape[2]), jnp.float32)
    for which in range(owned):
        hidden = jnp.dot(final_all, head_w1[which], preferred_element_type=jnp.float32)
        hidden = jax.nn.gelu(hidden + head_b1[which].astype(jnp.float32)).astype(jnp.bfloat16)
        answer = jnp.dot(hidden, head_w2[which], preferred_element_type=jnp.float32)
        result = jnp.where((kinds_all == first_kind + which)[:, None], answer, result)
    head_out = lax.psum_scatter(result, "type", scatter_dimension=0, tiled=True)
    return (updated, head_out)


def solution(mesh):
    seq = mesh.shape["seq"]
    kinds = mesh.shape["type"]
    y_n = 2
    x_n = 4
    z_n = seq // (x_n * y_n)
    split = Mesh(mesh.devices.reshape(z_n, x_n, y_n, kinds), ("z", "x", "y", "type"))
    rows = P(("z", "x", "y", "type"), None)
    in_specs = (
        rows,
        P(),
        P(),
        P(),
        P(None, None, "type"),
        P("type", None),
        rows,
        P("type", None, None),
        P("type", None),
        P("type", None, None),
    )
    out_specs = (rows, rows)
    return jax.shard_map(body, mesh=split, in_specs=in_specs, out_specs=out_specs, check_vma=False)
```

```python
import functools

import jax
import jax.numpy as jnp
from jax import lax
from jax.experimental import pallas as pl
from jax.experimental.pallas import tpu as pltpu
from jax.sharding import Mesh
from jax.sharding import PartitionSpec as P

HD = 64
SCALE = HD ** (-0.5)
QUERY_BLOCK = 544
ROW_SPLIT = 2
RING = ("z", "y")


def rms_normalize(values):
    squares = jnp.mean(values * values, axis=-1, keepdims=True)
    return values * lax.rsqrt(squares + 1e-06)


def step_kernel(first, last, *refs):
    if first:
        q_ref, kv_ref = refs[:2]
        rest = refs[2:]
    else:
        q_ref, kv_ref, m_in, l_in, acc_in = refs[:5]
        rest = refs[5:]
    m_s, l_s, acc_s = rest[-3:]
    outs = rest[:-3]
    if first:
        m_s[...] = jnp.full(m_s.shape, -jnp.inf, jnp.float32)
        l_s[...] = jnp.zeros(l_s.shape, jnp.float32)
        acc_s[...] = jnp.zeros(acc_s.shape, jnp.float32)
    else:
        m_s[...] = m_in[...]
        l_s[...] = l_in[...]
        acc_s[...] = acc_in[...]
    kv = kv_ref[...]
    rows = q_ref.shape[0] // ROW_SPLIT
    scores = []
    for g in range(ROW_SPLIT):
        scores.append(
            lax.dot_general(
                q_ref[g * rows : (g + 1) * rows, :],
                kv,
                (((1,), (1,)), ((), ())),
                preferred_element_type=jnp.float32,
            )
        )
    for g in range(ROW_SPLIT):
        part = slice(g * rows, (g + 1) * rows)
        m_old = m_s[part, :]
        m_new = jnp.maximum(m_old, jnp.max(scores[g], axis=1, keepdims=True))
        decay = jnp.exp(m_old - m_new)
        weights = jnp.exp(scores[g] - m_new)
        l_s[part, :] = decay * l_s[part, :] + jnp.sum(weights, axis=1, keepdims=True)
        acc_s[part, :] = decay * acc_s[part, :] + jnp.dot(
            weights.astype(jnp.bfloat16), kv, preferred_element_type=jnp.float32
        )
        m_s[part, :] = m_new
    if last:
        outs[0][...] = (acc_s[...] / l_s[...]).astype(outs[0].dtype)
    else:
        outs[0][...] = m_s[...]
        outs[1][...] = l_s[...]
        outs[2][...] = acc_s[...]


def flash_step(q_pad, kv, state, first, last):
    rows, width = q_pad.shape
    chunk = kv.shape[0]
    block = QUERY_BLOCK
    row_block = pl.BlockSpec((block, width), lambda i: (i, 0))
    stat_block = pl.BlockSpec((block, 1), lambda i: (i, 0))
    in_specs = [row_block, pl.BlockSpec((chunk, width), lambda i: (0, 0))]
    operands = [q_pad, kv]
    if not first:
        in_specs += [stat_block, stat_block, row_block]
        operands += list(state)
    if last:
        out_specs = row_block
        out_shape = jax.ShapeDtypeStruct((rows, width), jnp.bfloat16)
    else:
        out_specs = [stat_block, stat_block, row_block]
        out_shape = [
            jax.ShapeDtypeStruct((rows, 1), jnp.float32),
            jax.ShapeDtypeStruct((rows, 1), jnp.float32),
            jax.ShapeDtypeStruct((rows, width), jnp.float32),
        ]
    return pl.pallas_call(
        functools.partial(step_kernel, first, last),
        grid=(rows // block,),
        in_specs=in_specs,
        out_specs=out_specs,
        out_shape=out_shape,
        scratch_shapes=[
            pltpu.VMEM((block, 1), jnp.float32),
            pltpu.VMEM((block, 1), jnp.float32),
            pltpu.VMEM((block, width), jnp.float32),
        ],
        compiler_params=pltpu.CompilerParams(dimension_semantics=("arbitrary",)),
        cost_estimate=pl.CostEstimate(
            flops=4 * rows * chunk * width,
            transcendentals=rows * chunk,
            bytes_accessed=rows * width * 14 + chunk * width * 2,
        ),
    )(*operands)


def body(
    tokens, shift_scale, branch_gate, final_gain, w_qkv, w_out, type_ids, head_w1, head_b1, head_w2
):
    inputs = tokens.astype(jnp.float32)
    modulated = (rms_normalize(inputs) * (1.0 + shift_scale[1]) + shift_scale[0]).astype(
        jnp.bfloat16
    )
    gathered = lax.all_gather(modulated, "type", axis=0, tiled=True)
    dim = w_qkv.shape[1]
    local_heads = w_qkv.shape[2] // HD
    kinds = lax.axis_size("type")
    parts = w_qkv.reshape(3, dim, local_heads, HD)
    scaled = (parts[0] * SCALE).astype(parts.dtype)
    arranged = jnp.stack([scaled, jnp.zeros_like(scaled), parts[1], parts[2]], axis=2)
    arranged = arranged.reshape(dim, local_heads, 4 * HD)
    projected = jnp.einsum(
        "rd,dje->jre", gathered, arranged, preferred_element_type=jnp.float32
    ).astype(jnp.bfloat16)
    mine = lax.all_to_all(projected, "x", 0, 0, tiled=True)
    mine = mine.reshape(-1, 4 * HD)
    q_pad = mine[:, : 2 * HD]
    chunk = mine[:, 2 * HD :]
    w_out_dep, chunk = lax.optimization_barrier((w_out, chunk))
    w_out_all = lax.all_gather(w_out_dep, "type", axis=0, tiled=True)
    z_n = lax.axis_size("z")
    y_n = lax.axis_size("y")
    order = [z * y_n for z in range(z_n)] + [z * y_n + 1 for z in reversed(range(z_n))]
    if y_n != 2:
        order = list(range(z_n * y_n))
    pairs = [(order[i], order[(i + 1) % len(order)]) for i in range(len(order))]
    steps = len(order)
    state = None
    for step in range(steps):
        if step < steps - 1:
            coming = lax.ppermute(chunk, RING, pairs)
        state = flash_step(q_pad, chunk, state, step == 0, step == steps - 1)
        if step < steps - 1:
            chunk, state = lax.optimization_barrier((coming, state))
    attended = state[:, HD:]
    rows = tokens.shape[0]
    attended = attended.reshape(-1, kinds, rows, HD).reshape(-1, rows, HD)
    back = lax.all_to_all(attended, ("x", "type"), 0, 0, tiled=True)
    back = back.reshape(-1, kinds, rows, HD)
    back = jnp.transpose(back, (2, 1, 0, 3)).reshape(rows, -1)
    mixed = jnp.dot(back, w_out_all, preferred_element_type=jnp.float32)
    updated = (inputs + branch_gate * mixed).astype(jnp.bfloat16)
    final = (rms_normalize(updated.astype(jnp.float32)) * final_gain).astype(jnp.bfloat16)
    ids = jnp.broadcast_to(type_ids.astype(jnp.bfloat16), (rows, 128))
    joined = lax.all_gather(jnp.concatenate([final, ids], axis=1), "type", axis=0, tiled=True)
    final_all = joined[:, : final.shape[1]]
    kinds_all = joined[:, final.shape[1]].astype(jnp.int32)
    owned = head_w1.shape[0]
    first_kind = lax.axis_index("type") * owned
    result = jnp.zeros((final_all.shape[0], head_w2.shape[2]), jnp.float32)
    for which in range(owned):
        hidden = jnp.dot(final_all, head_w1[which], preferred_element_type=jnp.float32)
        hidden = jax.nn.gelu(hidden + head_b1[which].astype(jnp.float32)).astype(jnp.bfloat16)
        answer = jnp.dot(hidden, head_w2[which], preferred_element_type=jnp.float32)
        result = jnp.where((kinds_all == first_kind + which)[:, None], answer, result)
    head_out = lax.psum_scatter(result, "type", scatter_dimension=0, tiled=True)
    return (updated, head_out)


def solution(mesh):
    seq = mesh.shape["seq"]
    kinds = mesh.shape["type"]
    y_n = 2
    x_n = 4
    z_n = seq // (x_n * y_n)
    split = Mesh(mesh.devices.reshape(z_n, x_n, y_n, kinds), ("z", "x", "y", "type"))
    rows = P(("z", "x", "y", "type"), None)
    in_specs = (
        rows,
        P(),
        P(),
        P(),
        P(None, None, "type"),
        P("type", None),
        rows,
        P("type", None, None),
        P("type", None),
        P("type", None, None),
    )
    out_specs = (rows, rows)
    return jax.shard_map(body, mesh=split, in_specs=in_specs, out_specs=out_specs, check_vma=False)
```

```python
import functools

import jax
import jax.numpy as jnp
from jax import lax
from jax.experimental import pallas as pl
from jax.experimental.pallas import tpu as pltpu
from jax.sharding import Mesh
from jax.sharding import PartitionSpec as P

HD = 64
SCALE = HD ** (-0.5)
QUERY_BLOCK = 544
ROW_SPLIT = 2
RING = ("z", "y")


def rms_normalize(values):
    squares = jnp.mean(values * values, axis=-1, keepdims=True)
    return values * lax.rsqrt(squares + 1e-06)


def step_kernel(first, last, *refs):
    if first:
        q_ref, kv_ref = refs[:2]
        rest = refs[2:]
    else:
        q_ref, kv_ref, m_in, l_in, acc_in = refs[:5]
        rest = refs[5:]
    m_s, l_s, acc_s = rest[-3:]
    outs = rest[:-3]
    if first:
        m_s[...] = jnp.full(m_s.shape, -jnp.inf, jnp.float32)
        l_s[...] = jnp.zeros(l_s.shape, jnp.float32)
        acc_s[...] = jnp.zeros(acc_s.shape, jnp.float32)
    else:
        m_s[...] = m_in[...]
        l_s[...] = l_in[...]
        acc_s[...] = acc_in[...]
    kv = kv_ref[...]
    rows = q_ref.shape[0] // ROW_SPLIT
    scores = []
    for g in range(ROW_SPLIT):
        scores.append(
            lax.dot_general(
                q_ref[g * rows : (g + 1) * rows, :],
                kv,
                (((1,), (1,)), ((), ())),
                preferred_element_type=jnp.float32,
            )
        )
    for g in range(ROW_SPLIT):
        part = slice(g * rows, (g + 1) * rows)
        m_old = m_s[part, :]
        m_new = jnp.maximum(m_old, jnp.max(scores[g], axis=1, keepdims=True))
        decay = jnp.exp(m_old - m_new)
        weights = jnp.exp(scores[g] - m_new)
        l_s[part, :] = decay * l_s[part, :] + jnp.sum(weights, axis=1, keepdims=True)
        acc_s[part, :] = decay * acc_s[part, :] + jnp.dot(
            weights.astype(jnp.bfloat16), kv, preferred_element_type=jnp.float32
        )
        m_s[part, :] = m_new
    if last:
        outs[0][...] = (acc_s[...] / l_s[...]).astype(outs[0].dtype)
    else:
        outs[0][...] = m_s[...]
        outs[1][...] = l_s[...]
        outs[2][...] = acc_s[...]


def flash_step(q_pad, kv, state, first, last):
    rows, width = q_pad.shape
    chunk = kv.shape[0]
    block = QUERY_BLOCK
    row_block = pl.BlockSpec((block, width), lambda i: (i, 0))
    stat_block = pl.BlockSpec((block, 1), lambda i: (i, 0))
    in_specs = [row_block, pl.BlockSpec((chunk, width), lambda i: (0, 0))]
    operands = [q_pad, kv]
    if not first:
        in_specs += [stat_block, stat_block, row_block]
        operands += list(state)
    if last:
        out_specs = row_block
        out_shape = jax.ShapeDtypeStruct((rows, width), jnp.bfloat16)
    else:
        out_specs = [stat_block, stat_block, row_block]
        out_shape = [
            jax.ShapeDtypeStruct((rows, 1), jnp.float32),
            jax.ShapeDtypeStruct((rows, 1), jnp.float32),
            jax.ShapeDtypeStruct((rows, width), jnp.float32),
        ]
    return pl.pallas_call(
        functools.partial(step_kernel, first, last),
        grid=(rows // block,),
        in_specs=in_specs,
        out_specs=out_specs,
        out_shape=out_shape,
        scratch_shapes=[
            pltpu.VMEM((block, 1), jnp.float32),
            pltpu.VMEM((block, 1), jnp.float32),
            pltpu.VMEM((block, width), jnp.float32),
        ],
        compiler_params=pltpu.CompilerParams(dimension_semantics=("arbitrary",)),
        cost_estimate=pl.CostEstimate(
            flops=4 * rows * chunk * width,
            transcendentals=rows * chunk,
            bytes_accessed=rows * width * 14 + chunk * width * 2,
        ),
    )(*operands)


def from_each(pieces, axis):
    n = len(pieces)
    me = lax.axis_index(axis)
    turned = jnp.stack([pieces[(n - j) % n] for j in range(n)])
    return jnp.roll(turned, me, axis=0)


def gather_by_permutes(value, axis):
    n = lax.axis_size(axis)
    pieces = [value] + [
        lax.ppermute(value, axis, [(i, (i + k) % n) for i in range(n)]) for k in range(1, n)
    ]
    return from_each(pieces, axis)


def exchange_by_permutes(blocks, axis):
    n = lax.axis_size(axis)
    me = lax.axis_index(axis)
    pieces = [lax.dynamic_index_in_dim(blocks, me, 0, keepdims=False)]
    for k in range(1, n):
        send = lax.dynamic_index_in_dim(blocks, (me + k) % n, 0, keepdims=False)
        pieces.append(lax.ppermute(send, axis, [(i, (i + k) % n) for i in range(n)]))
    return from_each(pieces, axis)


def body(
    tokens, shift_scale, branch_gate, final_gain, w_qkv, w_out, type_ids, head_w1, head_b1, head_w2
):
    inputs = tokens.astype(jnp.float32)
    modulated = (rms_normalize(inputs) * (1.0 + shift_scale[1]) + shift_scale[0]).astype(
        jnp.bfloat16
    )
    gathered = gather_by_permutes(modulated, "type")
    gathered = gathered.reshape(-1, gathered.shape[-1])
    dim = w_qkv.shape[1]
    local_heads = w_qkv.shape[2] // HD
    kinds = lax.axis_size("type")
    parts = w_qkv.reshape(3, dim, local_heads, HD)
    scaled = (parts[0] * SCALE).astype(parts.dtype)
    arranged = jnp.stack([scaled, jnp.zeros_like(scaled), parts[1], parts[2]], axis=2)
    arranged = arranged.reshape(dim, local_heads, 4 * HD)
    projected = jnp.einsum(
        "rd,dje->jre", gathered, arranged, preferred_element_type=jnp.float32
    ).astype(jnp.bfloat16)
    mine = exchange_by_permutes(projected, "x")
    mine = mine.reshape(-1, 4 * HD)
    q_pad = mine[:, : 2 * HD]
    chunk = mine[:, 2 * HD :]
    w_out_dep, chunk = lax.optimization_barrier((w_out, chunk))
    w_out_all = lax.all_gather(w_out_dep, "type", axis=0, tiled=True)
    z_n = lax.axis_size("z")
    y_n = lax.axis_size("y")
    order = [z * y_n for z in range(z_n)] + [z * y_n + 1 for z in reversed(range(z_n))]
    if y_n != 2:
        order = list(range(z_n * y_n))
    n = len(order)
    right = [(order[i], order[(i + 1) % n]) for i in range(n)]
    left = [(order[i], order[(i - 1) % n]) for i in range(n)]
    plan = [[chunk]]
    state = None
    done = 0
    incoming = [lax.ppermute(chunk, RING, right), lax.ppermute(chunk, RING, left)]
    for d in range(n // 2 + 1):
        held = plan[-1] if d == 0 else incoming_now
        if d > 0:
            following = []
            if d + 1 <= n // 2:
                following.append(lax.ppermute(held[0], RING, right))
                if d + 1 < n - (d + 1):
                    following.append(lax.ppermute(held[1], RING, left))
        else:
            following = incoming
        for piece in held:
            state = flash_step(q_pad, piece, state, done == 0, done == n - 1)
            done += 1
        if following:
            incoming_now, state = lax.optimization_barrier((following, state))
    attended = state[:, HD:]
    rows = tokens.shape[0]
    attended = attended.reshape(-1, kinds, rows, HD).reshape(-1, rows, HD)
    back = lax.all_to_all(attended, ("x", "type"), 0, 0, tiled=True)
    back = back.reshape(-1, kinds, rows, HD)
    back = jnp.transpose(back, (2, 1, 0, 3)).reshape(rows, -1)
    mixed = jnp.dot(back, w_out_all, preferred_element_type=jnp.float32)
    updated = (inputs + branch_gate * mixed).astype(jnp.bfloat16)
    final = (rms_normalize(updated.astype(jnp.float32)) * final_gain).astype(jnp.bfloat16)
    ids = jnp.broadcast_to(type_ids.astype(jnp.bfloat16), (rows, 128))
    joined = lax.all_gather(jnp.concatenate([final, ids], axis=1), "type", axis=0, tiled=True)
    final_all = joined[:, : final.shape[1]]
    kinds_all = joined[:, final.shape[1]].astype(jnp.int32)
    owned = head_w1.shape[0]
    first_kind = lax.axis_index("type") * owned
    result = jnp.zeros((final_all.shape[0], head_w2.shape[2]), jnp.float32)
    for which in range(owned):
        hidden = jnp.dot(final_all, head_w1[which], preferred_element_type=jnp.float32)
        hidden = jax.nn.gelu(hidden + head_b1[which].astype(jnp.float32)).astype(jnp.bfloat16)
        answer = jnp.dot(hidden, head_w2[which], preferred_element_type=jnp.float32)
        result = jnp.where((kinds_all == first_kind + which)[:, None], answer, result)
    head_out = lax.psum_scatter(result, "type", scatter_dimension=0, tiled=True)
    return (updated, head_out)


def solution(mesh):
    seq = mesh.shape["seq"]
    kinds = mesh.shape["type"]
    y_n = 2
    x_n = 4
    z_n = seq // (x_n * y_n)
    split = Mesh(mesh.devices.reshape(z_n, x_n, y_n, kinds), ("z", "x", "y", "type"))
    rows = P(("z", "x", "y", "type"), None)
    in_specs = (
        rows,
        P(),
        P(),
        P(),
        P(None, None, "type"),
        P("type", None),
        rows,
        P("type", None, None),
        P("type", None),
        P("type", None, None),
    )
    out_specs = (rows, rows)
    return jax.shard_map(body, mesh=split, in_specs=in_specs, out_specs=out_specs, check_vma=False)
```

```python
import functools

import jax
import jax.numpy as jnp
from jax import lax
from jax.experimental import pallas as pl
from jax.experimental.pallas import tpu as pltpu
from jax.sharding import Mesh
from jax.sharding import PartitionSpec as P

HD = 64
SCALE = HD ** (-0.5)
QUERY_BLOCK = 544
ROW_SPLIT = 2
RING = ("z", "y")


def rms_normalize(values):
    squares = jnp.mean(values * values, axis=-1, keepdims=True)
    return values * lax.rsqrt(squares + 1e-06)


def step_kernel(first, last, *refs):
    if first:
        q_ref, kv_ref = refs[:2]
        rest = refs[2:]
    else:
        q_ref, kv_ref, m_in, l_in, acc_in = refs[:5]
        rest = refs[5:]
    m_s, l_s, acc_s = rest[-3:]
    outs = rest[:-3]
    if first:
        m_s[...] = jnp.full(m_s.shape, -jnp.inf, jnp.float32)
        l_s[...] = jnp.zeros(l_s.shape, jnp.float32)
        acc_s[...] = jnp.zeros(acc_s.shape, jnp.float32)
    else:
        m_s[...] = m_in[...]
        l_s[...] = l_in[...]
        acc_s[...] = acc_in[...]
    kv = kv_ref[...]
    rows = q_ref.shape[0] // ROW_SPLIT
    scores = []
    for g in range(ROW_SPLIT):
        scores.append(
            lax.dot_general(
                q_ref[g * rows : (g + 1) * rows, :],
                kv,
                (((1,), (1,)), ((), ())),
                preferred_element_type=jnp.float32,
            )
        )
    for g in range(ROW_SPLIT):
        part = slice(g * rows, (g + 1) * rows)
        m_old = m_s[part, :]
        m_new = jnp.maximum(m_old, jnp.max(scores[g], axis=1, keepdims=True))
        decay = jnp.exp(m_old - m_new)
        weights = jnp.exp(scores[g] - m_new)
        l_s[part, :] = decay * l_s[part, :] + jnp.sum(weights, axis=1, keepdims=True)
        acc_s[part, :] = decay * acc_s[part, :] + jnp.dot(
            weights.astype(jnp.bfloat16), kv, preferred_element_type=jnp.float32
        )
        m_s[part, :] = m_new
    if last:
        outs[0][...] = (acc_s[...] / l_s[...]).astype(outs[0].dtype)
    else:
        outs[0][...] = m_s[...]
        outs[1][...] = l_s[...]
        outs[2][...] = acc_s[...]


def flash_step(q_pad, kv, state, first, last):
    rows, width = q_pad.shape
    chunk = kv.shape[0]
    block = QUERY_BLOCK
    row_block = pl.BlockSpec((block, width), lambda i: (i, 0))
    stat_block = pl.BlockSpec((block, 1), lambda i: (i, 0))
    in_specs = [row_block, pl.BlockSpec((chunk, width), lambda i: (0, 0))]
    operands = [q_pad, kv]
    if not first:
        in_specs += [stat_block, stat_block, row_block]
        operands += list(state)
    if last:
        out_specs = row_block
        out_shape = jax.ShapeDtypeStruct((rows, width), jnp.bfloat16)
    else:
        out_specs = [stat_block, stat_block, row_block]
        out_shape = [
            jax.ShapeDtypeStruct((rows, 1), jnp.float32),
            jax.ShapeDtypeStruct((rows, 1), jnp.float32),
            jax.ShapeDtypeStruct((rows, width), jnp.float32),
        ]
    return pl.pallas_call(
        functools.partial(step_kernel, first, last),
        grid=(rows // block,),
        in_specs=in_specs,
        out_specs=out_specs,
        out_shape=out_shape,
        scratch_shapes=[
            pltpu.VMEM((block, 1), jnp.float32),
            pltpu.VMEM((block, 1), jnp.float32),
            pltpu.VMEM((block, width), jnp.float32),
        ],
        compiler_params=pltpu.CompilerParams(dimension_semantics=("arbitrary",)),
        cost_estimate=pl.CostEstimate(
            flops=4 * rows * chunk * width,
            transcendentals=rows * chunk,
            bytes_accessed=rows * width * 14 + chunk * width * 2,
        ),
    )(*operands)


def shifted(value, axis, k):
    n = lax.axis_size(axis)
    return lax.ppermute(value, axis, [(i, (i + k) % n) for i in range(n)])

def body(
    tokens, shift_scale, branch_gate, final_gain, w_qkv, w_out, type_ids, head_w1, head_b1, head_w2
):
    inputs = tokens.astype(jnp.float32)
    modulated = (rms_normalize(inputs) * (1.0 + shift_scale[1]) + shift_scale[0]).astype(
        jnp.bfloat16
    )
    kinds = lax.axis_size("type")
    gathered = jnp.concatenate(
        [modulated] + [shifted(modulated, "type", k) for k in range(1, kinds)], axis=0
    )
    dim = w_qkv.shape[1]
    local_heads = w_qkv.shape[2] // HD
    parts = w_qkv.reshape(3, dim, local_heads, HD)
    scaled = (parts[0] * SCALE).astype(parts.dtype)
    arranged = jnp.stack([scaled, jnp.zeros_like(scaled), parts[1], parts[2]], axis=2)
    arranged = arranged.reshape(dim, local_heads, 4 * HD)
    arranged = jnp.roll(arranged, -lax.axis_index("x"), axis=1)
    projected = jnp.einsum(
        "rd,dje->jre", gathered, arranged, preferred_element_type=jnp.float32
    ).astype(jnp.bfloat16)
    mine = jnp.concatenate(
        [projected[0]] + [shifted(projected[k], "x", k) for k in range(1, local_heads)], axis=0
    )
    q_pad = mine[:, : 2 * HD]
    chunk = mine[:, 2 * HD :]
    w_out_dep, chunk = lax.optimization_barrier((w_out, chunk))
    w_out_all = lax.all_gather(w_out_dep, "type", axis=0, tiled=True)
    z_n = lax.axis_size("z")
    y_n = lax.axis_size("y")
    order = [z * y_n for z in range(z_n)] + [z * y_n + 1 for z in reversed(range(z_n))]
    if y_n != 2:
        order = list(range(z_n * y_n))
    n = len(order)
    right = [(order[i], order[(i + 1) % n]) for i in range(n)]
    left = [(order[i], order[(i - 1) % n]) for i in range(n)]
    plan = [[chunk]]
    state = None
    done = 0
    incoming = [lax.ppermute(chunk, RING, right), lax.ppermute(chunk, RING, left)]
    for d in range(n // 2 + 1):
        held = plan[-1] if d == 0 else incoming_now
        if d > 0:
            following = []
            if d + 1 <= n // 2:
                following.append(lax.ppermute(held[0], RING, right))
                if d + 1 < n - (d + 1):
                    following.append(lax.ppermute(held[1], RING, left))
        else:
            following = incoming
        for piece in held:
            state = flash_step(q_pad, piece, state, done == 0, done == n - 1)
            done += 1
        if following:
            incoming_now, state = lax.optimization_barrier((following, state))
    attended = state[:, HD:]
    rows = tokens.shape[0]
    attended = attended.reshape(-1, rows, HD)
    owner = jnp.arange(local_heads * kinds)
    pick = ((lax.axis_index("x") - owner // kinds) % local_heads) * kinds + (
        lax.axis_index("type") - owner % kinds
    ) % kinds
    attended = jnp.take(attended, pick, axis=0)
    back = lax.all_to_all(attended, ("x", "type"), 0, 0, tiled=True)
    back = back.reshape(-1, kinds, rows, HD)
    back = jnp.transpose(back, (2, 1, 0, 3)).reshape(rows, -1)
    mixed = jnp.dot(back, w_out_all, preferred_element_type=jnp.float32)
    updated = (inputs + branch_gate * mixed).astype(jnp.bfloat16)
    final = (rms_normalize(updated.astype(jnp.float32)) * final_gain).astype(jnp.bfloat16)
    ids = jnp.broadcast_to(type_ids.astype(jnp.bfloat16), (rows, 128))
    ext = jnp.concatenate([final, ids], axis=1)
    joined = jnp.concatenate([ext] + [shifted(ext, "type", k) for k in range(1, kinds)], axis=0)
    final_all = joined[:, : final.shape[1]]
    kinds_all = joined[:, final.shape[1]].astype(jnp.int32)
    owned = head_w1.shape[0]
    first_kind = lax.axis_index("type") * owned
    result = jnp.zeros((final_all.shape[0], head_w2.shape[2]), jnp.float32)
    for which in range(owned):
        hidden = jnp.dot(final_all, head_w1[which], preferred_element_type=jnp.float32)
        hidden = jax.nn.gelu(hidden + head_b1[which].astype(jnp.float32)).astype(jnp.bfloat16)
        answer = jnp.dot(hidden, head_w2[which], preferred_element_type=jnp.float32)
        result = jnp.where((kinds_all == first_kind + which)[:, None], answer, result)
    result = result.reshape(kinds, rows, -1)
    head_out = result[0]
    for k in range(1, kinds):
        head_out = head_out + shifted(result[(-k) % kinds], "type", k)
    return (updated, head_out)


def solution(mesh):
    seq = mesh.shape["seq"]
    kinds = mesh.shape["type"]
    y_n = 2
    x_n = 4
    z_n = seq // (x_n * y_n)
    split = Mesh(mesh.devices.reshape(z_n, x_n, y_n, kinds), ("z", "x", "y", "type"))
    rows = P(("z", "x", "y", "type"), None)
    in_specs = (
        rows,
        P(),
        P(),
        P(),
        P(None, None, "type"),
        P("type", None),
        rows,
        P("type", None, None),
        P("type", None),
        P("type", None, None),
    )
    out_specs = (rows, rows)
    return jax.shard_map(body, mesh=split, in_specs=in_specs, out_specs=out_specs, check_vma=False)
```

```python
import functools

import jax
import jax.numpy as jnp
from jax import lax
from jax.experimental import pallas as pl
from jax.experimental.pallas import tpu as pltpu
from jax.sharding import Mesh
from jax.sharding import PartitionSpec as P

HD = 64
SCALE = HD ** (-0.5)
QUERY_BLOCK = 544
ROW_SPLIT = 2


def rms_normalize(values):
    squares = jnp.mean(values * values, axis=-1, keepdims=True)
    return values * lax.rsqrt(squares + 1e-06)


def step_kernel(first, last, *refs):
    if first:
        q_ref, kv_ref = refs[:2]
        rest = refs[2:]
    else:
        q_ref, kv_ref, m_in, l_in, acc_in = refs[:5]
        rest = refs[5:]
    m_s, l_s, acc_s = rest[-3:]
    outs = rest[:-3]
    if first:
        m_s[...] = jnp.full(m_s.shape, -jnp.inf, jnp.float32)
        l_s[...] = jnp.zeros(l_s.shape, jnp.float32)
        acc_s[...] = jnp.zeros(acc_s.shape, jnp.float32)
    else:
        m_s[...] = m_in[...]
        l_s[...] = l_in[...]
        acc_s[...] = acc_in[...]
    kv = kv_ref[...]
    rows = q_ref.shape[0] // ROW_SPLIT
    scores = []
    for g in range(ROW_SPLIT):
        scores.append(
            lax.dot_general(
                q_ref[g * rows : (g + 1) * rows, :],
                kv,
                (((1,), (1,)), ((), ())),
                preferred_element_type=jnp.float32,
            )
        )
    for g in range(ROW_SPLIT):
        part = slice(g * rows, (g + 1) * rows)
        m_old = m_s[part, :]
        m_new = jnp.maximum(m_old, jnp.max(scores[g], axis=1, keepdims=True))
        decay = jnp.exp(m_old - m_new)
        weights = jnp.exp(scores[g] - m_new)
        l_s[part, :] = decay * l_s[part, :] + jnp.sum(weights, axis=1, keepdims=True)
        acc_s[part, :] = decay * acc_s[part, :] + jnp.dot(
            weights.astype(jnp.bfloat16), kv, preferred_element_type=jnp.float32
        )
        m_s[part, :] = m_new
    if last:
        outs[0][...] = (acc_s[...] / l_s[...]).astype(outs[0].dtype)
    else:
        outs[0][...] = m_s[...]
        outs[1][...] = l_s[...]
        outs[2][...] = acc_s[...]


def flash_step(q_pad, kv, state, first, last):
    rows, width = q_pad.shape
    chunk = kv.shape[0]
    block = QUERY_BLOCK
    row_block = pl.BlockSpec((block, width), lambda i: (i, 0))
    stat_block = pl.BlockSpec((block, 1), lambda i: (i, 0))
    in_specs = [row_block, pl.BlockSpec((chunk, width), lambda i: (0, 0))]
    operands = [q_pad, kv]
    if not first:
        in_specs += [stat_block, stat_block, row_block]
        operands += list(state)
    if last:
        out_specs = row_block
        out_shape = jax.ShapeDtypeStruct((rows, width), jnp.bfloat16)
    else:
        out_specs = [stat_block, stat_block, row_block]
        out_shape = [
            jax.ShapeDtypeStruct((rows, 1), jnp.float32),
            jax.ShapeDtypeStruct((rows, 1), jnp.float32),
            jax.ShapeDtypeStruct((rows, width), jnp.float32),
        ]
    return pl.pallas_call(
        functools.partial(step_kernel, first, last),
        grid=(rows // block,),
        in_specs=in_specs,
        out_specs=out_specs,
        out_shape=out_shape,
        scratch_shapes=[
            pltpu.VMEM((block, 1), jnp.float32),
            pltpu.VMEM((block, 1), jnp.float32),
            pltpu.VMEM((block, width), jnp.float32),
        ],
        compiler_params=pltpu.CompilerParams(dimension_semantics=("arbitrary",)),
        cost_estimate=pl.CostEstimate(
            flops=4 * rows * chunk * width,
            transcendentals=rows * chunk,
            bytes_accessed=rows * width * 14 + chunk * width * 2,
        ),
    )(*operands)


def shifted(value, axis, k):
    n = lax.axis_size(axis)
    return lax.ppermute(value, axis, [(i, (i + k) % n) for i in range(n)])

def body(
    tokens, shift_scale, branch_gate, final_gain, w_qkv, w_out, type_ids, head_w1, head_b1, head_w2
):
    inputs = tokens.astype(jnp.float32)
    modulated = (rms_normalize(inputs) * (1.0 + shift_scale[1]) + shift_scale[0]).astype(
        jnp.bfloat16
    )
    kinds = lax.axis_size("type")
    gathered = jnp.concatenate(
        [modulated] + [shifted(modulated, "type", k) for k in range(1, kinds)], axis=0
    )
    dim = w_qkv.shape[1]
    local_heads = w_qkv.shape[2] // HD
    parts = w_qkv.reshape(3, dim, local_heads, HD)
    scaled = (parts[0] * SCALE).astype(parts.dtype)
    arranged = jnp.stack([scaled, jnp.zeros_like(scaled), parts[1], parts[2]], axis=2)
    arranged = arranged.reshape(dim, local_heads, 4 * HD)
    arranged = jnp.roll(arranged, -lax.axis_index("x"), axis=1)
    projected = jnp.einsum(
        "rd,dje->jre", gathered, arranged, preferred_element_type=jnp.float32
    ).astype(jnp.bfloat16)
    mine = jnp.concatenate(
        [projected[0]] + [shifted(projected[k], "x", k) for k in range(1, local_heads)], axis=0
    )
    q_pad = mine[:, : 2 * HD]
    chunk = mine[:, 2 * HD :]
    z_n = lax.axis_size("z")
    zr = [(i, (i + 1) % z_n) for i in range(z_n)]
    zl = [(i, (i - 1) % z_n) for i in range(z_n)]
    yy = [(0, 1), (1, 0)]
    held = [chunk]
    state = None
    done = 0
    total = 2 * z_n
    w_out_all = None
    for stage in range(4):
        if stage == 0:
            following = [
                lax.ppermute(chunk, "z", zr),
                lax.ppermute(chunk, "z", zl),
                lax.ppermute(chunk, "y", yy),
            ]
        elif stage == 1:
            following = [
                lax.ppermute(held[0], "z", zr),
                lax.ppermute(held[2], "z", zr),
                lax.ppermute(held[2], "z", zl),
            ]
        elif stage == 2:
            following = [lax.ppermute(held[1], "z", zr)]
        else:
            following = []
        for piece in held:
            state = flash_step(q_pad, piece, state, done == 0, done == total - 1)
            done += 1
        if following:
            held, state = lax.optimization_barrier((following, state))
        if stage == 0:
            w_out_dep, held = lax.optimization_barrier((w_out, held))
            w_out_all = lax.all_gather(w_out_dep, "type", axis=0, tiled=True)
    attended = state[:, HD:]
    rows = tokens.shape[0]
    attended = attended.reshape(-1, rows, HD)
    owner = jnp.arange(local_heads * kinds)
    pick = ((lax.axis_index("x") - owner // kinds) % local_heads) * kinds + (
        lax.axis_index("type") - owner % kinds
    ) % kinds
    attended = jnp.take(attended, pick, axis=0)
    back = lax.all_to_all(attended, ("x", "type"), 0, 0, tiled=True)
    back = back.reshape(-1, kinds, rows, HD)
    back = jnp.transpose(back, (2, 1, 0, 3)).reshape(rows, -1)
    mixed = jnp.dot(back, w_out_all, preferred_element_type=jnp.float32)
    updated = (inputs + branch_gate * mixed).astype(jnp.bfloat16)
    final = (rms_normalize(updated.astype(jnp.float32)) * final_gain).astype(jnp.bfloat16)
    ids = jnp.broadcast_to(type_ids.astype(jnp.bfloat16), (rows, 128))
    ext = jnp.concatenate([final, ids], axis=1)
    joined = jnp.concatenate([ext] + [shifted(ext, "type", k) for k in range(1, kinds)], axis=0)
    final_all = joined[:, : final.shape[1]]
    kinds_all = joined[:, final.shape[1]].astype(jnp.int32)
    owned = head_w1.shape[0]
    first_kind = lax.axis_index("type") * owned
    result = jnp.zeros((final_all.shape[0], head_w2.shape[2]), jnp.float32)
    for which in range(owned):
        hidden = jnp.dot(final_all, head_w1[which], preferred_element_type=jnp.float32)
        hidden = jax.nn.gelu(hidden + head_b1[which].astype(jnp.float32)).astype(jnp.bfloat16)
        answer = jnp.dot(hidden, head_w2[which], preferred_element_type=jnp.float32)
        result = jnp.where((kinds_all == first_kind + which)[:, None], answer, result)
    result = result.reshape(kinds, rows, -1)
    head_out = result[0]
    for k in range(1, kinds):
        head_out = head_out + shifted(result[(-k) % kinds], "type", k)
    return (updated, head_out)


def solution(mesh):
    seq = mesh.shape["seq"]
    kinds = mesh.shape["type"]
    y_n = 2
    x_n = 4
    z_n = seq // (x_n * y_n)
    split = Mesh(mesh.devices.reshape(z_n, x_n, y_n, kinds), ("z", "x", "y", "type"))
    rows = P(("z", "x", "y", "type"), None)
    in_specs = (
        rows,
        P(),
        P(),
        P(),
        P(None, None, "type"),
        P("type", None),
        rows,
        P("type", None, None),
        P("type", None),
        P("type", None, None),
    )
    out_specs = (rows, rows)
    return jax.shard_map(body, mesh=split, in_specs=in_specs, out_specs=out_specs, check_vma=False)
```

```python
import functools

import jax
import jax.numpy as jnp
from jax import lax
from jax.experimental import pallas as pl
from jax.experimental.pallas import tpu as pltpu
from jax.sharding import Mesh
from jax.sharding import PartitionSpec as P

HD = 64
SCALE = HD ** (-0.5)
QUERY_BLOCK = 544
ROW_SPLIT = 2


def rms_normalize(values):
    squares = jnp.mean(values * values, axis=-1, keepdims=True)
    return values * lax.rsqrt(squares + 1e-06)


def step_kernel(first, last, *refs):
    if first:
        q_ref, kv_ref = refs[:2]
        rest = refs[2:]
    else:
        q_ref, kv_ref, m_in, l_in, acc_in = refs[:5]
        rest = refs[5:]
    m_s, l_s, acc_s = rest[-3:]
    outs = rest[:-3]
    chunk = pl.program_id(1)

    @pl.when(chunk == 0)
    def _():
        if first:
            m_s[...] = jnp.full(m_s.shape, -jnp.inf, jnp.float32)
            l_s[...] = jnp.zeros(l_s.shape, jnp.float32)
            acc_s[...] = jnp.zeros(acc_s.shape, jnp.float32)
        else:
            m_s[...] = m_in[...]
            l_s[...] = l_in[...]
            acc_s[...] = acc_in[...]

    kv = kv_ref[...]
    rows = q_ref.shape[0] // ROW_SPLIT
    scores = []
    for g in range(ROW_SPLIT):
        scores.append(
            lax.dot_general(
                q_ref[g * rows : (g + 1) * rows, :],
                kv,
                (((1,), (1,)), ((), ())),
                preferred_element_type=jnp.float32,
            )
        )
    for g in range(ROW_SPLIT):
        part = slice(g * rows, (g + 1) * rows)
        m_old = m_s[part, :]
        m_new = jnp.maximum(m_old, jnp.max(scores[g], axis=1, keepdims=True))
        decay = jnp.exp(m_old - m_new)
        weights = jnp.exp(scores[g] - m_new)
        l_s[part, :] = decay * l_s[part, :] + jnp.sum(weights, axis=1, keepdims=True)
        acc_s[part, :] = decay * acc_s[part, :] + jnp.dot(
            weights.astype(jnp.bfloat16), kv, preferred_element_type=jnp.float32
        )
        m_s[part, :] = m_new

    @pl.when(chunk == pl.num_programs(1) - 1)
    def _():
        if last:
            outs[0][...] = (acc_s[...] / l_s[...]).astype(outs[0].dtype)
        else:
            outs[0][...] = m_s[...]
            outs[1][...] = l_s[...]
            outs[2][...] = acc_s[...]


def flash_step(q_pad, kv, state, first, last):
    rows, width = q_pad.shape
    chunks, chunk = kv.shape[:2]
    block = QUERY_BLOCK
    row_block = pl.BlockSpec((block, width), lambda i, c: (i, 0))
    stat_block = pl.BlockSpec((block, 1), lambda i, c: (i, 0))
    in_specs = [row_block, pl.BlockSpec((None, chunk, width), lambda i, c: (c, 0, 0))]
    operands = [q_pad, kv]
    if not first:
        in_specs += [stat_block, stat_block, row_block]
        operands += list(state)
    if last:
        out_specs = row_block
        out_shape = jax.ShapeDtypeStruct((rows, width), jnp.bfloat16)
    else:
        out_specs = [stat_block, stat_block, row_block]
        out_shape = [
            jax.ShapeDtypeStruct((rows, 1), jnp.float32),
            jax.ShapeDtypeStruct((rows, 1), jnp.float32),
            jax.ShapeDtypeStruct((rows, width), jnp.float32),
        ]
    return pl.pallas_call(
        functools.partial(step_kernel, first, last),
        grid=(rows // block, chunks),
        in_specs=in_specs,
        out_specs=out_specs,
        out_shape=out_shape,
        scratch_shapes=[
            pltpu.VMEM((block, 1), jnp.float32),
            pltpu.VMEM((block, 1), jnp.float32),
            pltpu.VMEM((block, width), jnp.float32),
        ],
        compiler_params=pltpu.CompilerParams(dimension_semantics=("arbitrary", "arbitrary")),
        cost_estimate=pl.CostEstimate(
            flops=4 * rows * chunks * chunk * width,
            transcendentals=rows * chunks * chunk,
            bytes_accessed=rows * width * 14 + (rows // block) * chunks * chunk * width * 2,
        ),
    )(*operands)


def shifted(value, axis, k):
    n = lax.axis_size(axis)
    return lax.ppermute(value, axis, [(i, (i + k) % n) for i in range(n)])

def body(
    tokens, shift_scale, branch_gate, final_gain, w_qkv, w_out, type_ids, head_w1, head_b1, head_w2
):
    inputs = tokens.astype(jnp.float32)
    modulated = (rms_normalize(inputs) * (1.0 + shift_scale[1]) + shift_scale[0]).astype(
        jnp.bfloat16
    )
    kinds = lax.axis_size("type")
    gathered = jnp.concatenate(
        [modulated] + [shifted(modulated, "type", k) for k in range(1, kinds)], axis=0
    )
    dim = w_qkv.shape[1]
    local_heads = w_qkv.shape[2] // HD
    parts = w_qkv.reshape(3, dim, local_heads, HD)
    scaled = (parts[0] * SCALE).astype(parts.dtype)
    arranged = jnp.stack([scaled, jnp.zeros_like(scaled), parts[1], parts[2]], axis=2)
    arranged = arranged.reshape(dim, local_heads, 4 * HD)
    arranged = jnp.roll(arranged, -lax.axis_index("x"), axis=1)
    projected = jnp.einsum(
        "rd,dje->jre", gathered, arranged, preferred_element_type=jnp.float32
    ).astype(jnp.bfloat16)
    mine = jnp.concatenate(
        [projected[0]] + [shifted(projected[k], "x", k) for k in range(1, local_heads)], axis=0
    )
    q_pad = mine[:, : 2 * HD]
    chunk = mine[:, 2 * HD :]
    z_n = lax.axis_size("z")
    zr = [(i, (i + 1) % z_n) for i in range(z_n)]
    zl = [(i, (i - 1) % z_n) for i in range(z_n)]
    yy = [(0, 1), (1, 0)]
    held = [chunk]
    state = None
    w_out_all = None
    for stage in range(4):
        if stage == 0:
            following = [
                lax.ppermute(chunk, "z", zr),
                lax.ppermute(chunk, "z", zl),
                lax.ppermute(chunk, "y", yy),
            ]
        elif stage == 1:
            following = [
                lax.ppermute(held[0], "z", zr),
                lax.ppermute(held[2], "z", zr),
                lax.ppermute(held[2], "z", zl),
            ]
        elif stage == 2:
            following = [lax.ppermute(held[1], "z", zr)]
        else:
            following = []
        state = flash_step(q_pad, jnp.stack(held), state, stage == 0, stage == 3)
        if following:
            held, state = lax.optimization_barrier((following, state))
        if stage == 0:
            w_out_dep, held = lax.optimization_barrier((w_out, held))
            w_out_all = lax.all_gather(w_out_dep, "type", axis=0, tiled=True)
    attended = state[:, HD:]
    rows = tokens.shape[0]
    attended = attended.reshape(-1, rows, HD)
    owner = jnp.arange(local_heads * kinds)
    pick = ((lax.axis_index("x") - owner // kinds) % local_heads) * kinds + (
        lax.axis_index("type") - owner % kinds
    ) % kinds
    attended = jnp.take(attended, pick, axis=0)
    back = lax.all_to_all(attended, ("x", "type"), 0, 0, tiled=True)
    back = back.reshape(-1, kinds, rows, HD)
    back = jnp.transpose(back, (2, 1, 0, 3)).reshape(rows, -1)
    mixed = jnp.dot(back, w_out_all, preferred_element_type=jnp.float32)
    updated = (inputs + branch_gate * mixed).astype(jnp.bfloat16)
    final = (rms_normalize(updated.astype(jnp.float32)) * final_gain).astype(jnp.bfloat16)
    ids = jnp.broadcast_to(type_ids.astype(jnp.bfloat16), (rows, 128))
    ext = jnp.concatenate([final, ids], axis=1)
    joined = jnp.concatenate([ext] + [shifted(ext, "type", k) for k in range(1, kinds)], axis=0)
    final_all = joined[:, : final.shape[1]]
    kinds_all = joined[:, final.shape[1]].astype(jnp.int32)
    owned = head_w1.shape[0]
    first_kind = lax.axis_index("type") * owned
    result = jnp.zeros((final_all.shape[0], head_w2.shape[2]), jnp.float32)
    for which in range(owned):
        hidden = jnp.dot(final_all, head_w1[which], preferred_element_type=jnp.float32)
        hidden = jax.nn.gelu(hidden + head_b1[which].astype(jnp.float32)).astype(jnp.bfloat16)
        answer = jnp.dot(hidden, head_w2[which], preferred_element_type=jnp.float32)
        result = jnp.where((kinds_all == first_kind + which)[:, None], answer, result)
    result = result.reshape(kinds, rows, -1)
    head_out = result[0]
    for k in range(1, kinds):
        head_out = head_out + shifted(result[(-k) % kinds], "type", k)
    return (updated, head_out)


def solution(mesh):
    seq = mesh.shape["seq"]
    kinds = mesh.shape["type"]
    y_n = 2
    x_n = 4
    z_n = seq // (x_n * y_n)
    split = Mesh(mesh.devices.reshape(z_n, x_n, y_n, kinds), ("z", "x", "y", "type"))
    rows = P(("z", "x", "y", "type"), None)
    in_specs = (
        rows,
        P(),
        P(),
        P(),
        P(None, None, "type"),
        P("type", None),
        rows,
        P("type", None, None),
        P("type", None),
        P("type", None, None),
    )
    out_specs = (rows, rows)
    return jax.shard_map(body, mesh=split, in_specs=in_specs, out_specs=out_specs, check_vma=False)
```

```python
import functools

import jax
import jax.numpy as jnp
from jax import lax
from jax.experimental import pallas as pl
from jax.experimental.pallas import tpu as pltpu
from jax.sharding import Mesh
from jax.sharding import PartitionSpec as P

HD = 64
SCALE = HD ** (-0.5)
QUERY_BLOCK = 544
ROW_SPLIT = 2


def rms_normalize(values):
    squares = jnp.mean(values * values, axis=-1, keepdims=True)
    return values * lax.rsqrt(squares + 1e-06)


def step_kernel(first, last, *refs):
    if first:
        q_ref, kv_ref = refs[:2]
        rest = refs[2:]
    else:
        q_ref, kv_ref, m_in, l_in, acc_in = refs[:5]
        rest = refs[5:]
    m_s, l_s, acc_s = rest[-3:]
    outs = rest[:-3]
    chunk = pl.program_id(1)

    @pl.when(chunk == 0)
    def _():
        if first:
            m_s[...] = jnp.full(m_s.shape, -jnp.inf, jnp.float32)
            l_s[...] = jnp.zeros(l_s.shape, jnp.float32)
            acc_s[...] = jnp.zeros(acc_s.shape, jnp.float32)
        else:
            m_s[...] = m_in[...]
            l_s[...] = l_in[...]
            acc_s[...] = acc_in[...]

    kv = kv_ref[...]
    lane = lax.broadcasted_iota(jnp.int32, kv.shape, 1)
    kv_sums = jnp.where(lane < HD, jnp.ones_like(kv), kv)
    rows = q_ref.shape[0] // ROW_SPLIT
    scores = []
    for g in range(ROW_SPLIT):
        scores.append(
            lax.dot_general(
                q_ref[g * rows : (g + 1) * rows, :],
                kv,
                (((1,), (1,)), ((), ())),
                preferred_element_type=jnp.float32,
            )
        )
    for g in range(ROW_SPLIT):
        part = slice(g * rows, (g + 1) * rows)
        m_old = m_s[part, :]
        m_new = jnp.maximum(m_old, jnp.max(scores[g], axis=1, keepdims=True))
        decay = jnp.exp(m_old - m_new)
        weights = jnp.exp(scores[g] - m_new).astype(jnp.bfloat16)
        acc_s[part, :] = decay * acc_s[part, :] + jnp.dot(
            weights, kv_sums, preferred_element_type=jnp.float32
        )
        m_s[part, :] = m_new

    @pl.when(chunk == pl.num_programs(1) - 1)
    def _():
        if last:
            outs[0][...] = (acc_s[...] / acc_s[:, 0:1]).astype(outs[0].dtype)
        else:
            outs[0][...] = m_s[...]
            outs[1][...] = l_s[...]
            outs[2][...] = acc_s[...]


def flash_step(q_pad, kv, state, first, last):
    rows, width = q_pad.shape
    chunks, chunk = kv.shape[:2]
    block = QUERY_BLOCK
    row_block = pl.BlockSpec((block, width), lambda i, c: (i, 0))
    stat_block = pl.BlockSpec((block, 1), lambda i, c: (i, 0))
    in_specs = [row_block, pl.BlockSpec((None, chunk, width), lambda i, c: (c, 0, 0))]
    operands = [q_pad, kv]
    if not first:
        in_specs += [stat_block, stat_block, row_block]
        operands += list(state)
    if last:
        out_specs = row_block
        out_shape = jax.ShapeDtypeStruct((rows, width), jnp.bfloat16)
    else:
        out_specs = [stat_block, stat_block, row_block]
        out_shape = [
            jax.ShapeDtypeStruct((rows, 1), jnp.float32),
            jax.ShapeDtypeStruct((rows, 1), jnp.float32),
            jax.ShapeDtypeStruct((rows, width), jnp.float32),
        ]
    return pl.pallas_call(
        functools.partial(step_kernel, first, last),
        grid=(rows // block, chunks),
        in_specs=in_specs,
        out_specs=out_specs,
        out_shape=out_shape,
        scratch_shapes=[
            pltpu.VMEM((block, 1), jnp.float32),
            pltpu.VMEM((block, 1), jnp.float32),
            pltpu.VMEM((block, width), jnp.float32),
        ],
        compiler_params=pltpu.CompilerParams(dimension_semantics=("arbitrary", "arbitrary")),
        cost_estimate=pl.CostEstimate(
            flops=4 * rows * chunks * chunk * width,
            transcendentals=rows * chunks * chunk,
            bytes_accessed=rows * width * 14 + (rows // block) * chunks * chunk * width * 2,
        ),
    )(*operands)


def shifted(value, axis, k):
    n = lax.axis_size(axis)
    return lax.ppermute(value, axis, [(i, (i + k) % n) for i in range(n)])

def body(
    tokens, shift_scale, branch_gate, final_gain, w_qkv, w_out, type_ids, head_w1, head_b1, head_w2
):
    inputs = tokens.astype(jnp.float32)
    modulated = (rms_normalize(inputs) * (1.0 + shift_scale[1]) + shift_scale[0]).astype(
        jnp.bfloat16
    )
    kinds = lax.axis_size("type")
    gathered = jnp.concatenate(
        [modulated] + [shifted(modulated, "type", k) for k in range(1, kinds)], axis=0
    )
    dim = w_qkv.shape[1]
    local_heads = w_qkv.shape[2] // HD
    parts = w_qkv.reshape(3, dim, local_heads, HD)
    scaled = (parts[0] * SCALE).astype(parts.dtype)
    arranged = jnp.stack([scaled, jnp.zeros_like(scaled), parts[1], parts[2]], axis=2)
    arranged = arranged.reshape(dim, local_heads, 4 * HD)
    arranged = jnp.roll(arranged, -lax.axis_index("x"), axis=1)
    projected = jnp.einsum(
        "rd,dje->jre", gathered, arranged, preferred_element_type=jnp.float32
    ).astype(jnp.bfloat16)
    mine = jnp.concatenate(
        [projected[0]] + [shifted(projected[k], "x", k) for k in range(1, local_heads)], axis=0
    )
    q_pad = mine[:, : 2 * HD]
    chunk = mine[:, 2 * HD :]
    z_n = lax.axis_size("z")
    zr = [(i, (i + 1) % z_n) for i in range(z_n)]
    zl = [(i, (i - 1) % z_n) for i in range(z_n)]
    yy = [(0, 1), (1, 0)]
    held = [chunk]
    state = None
    w_out_all = None
    for stage in range(4):
        if stage == 0:
            following = [
                lax.ppermute(chunk, "z", zr),
                lax.ppermute(chunk, "z", zl),
                lax.ppermute(chunk, "y", yy),
            ]
        elif stage == 1:
            following = [
                lax.ppermute(held[0], "z", zr),
                lax.ppermute(held[2], "z", zr),
                lax.ppermute(held[2], "z", zl),
            ]
        elif stage == 2:
            following = [lax.ppermute(held[1], "z", zr)]
        else:
            following = []
        state = flash_step(q_pad, jnp.stack(held), state, stage == 0, stage == 3)
        if following:
            held, state = lax.optimization_barrier((following, state))
        if stage == 0:
            w_out_dep, held = lax.optimization_barrier((w_out, held))
            w_out_all = lax.all_gather(w_out_dep, "type", axis=0, tiled=True)
    attended = state[:, HD:]
    rows = tokens.shape[0]
    attended = attended.reshape(-1, rows, HD)
    owner = jnp.arange(local_heads * kinds)
    pick = ((lax.axis_index("x") - owner // kinds) % local_heads) * kinds + (
        lax.axis_index("type") - owner % kinds
    ) % kinds
    attended = jnp.take(attended, pick, axis=0)
    back = lax.all_to_all(attended, ("x", "type"), 0, 0, tiled=True)
    back = back.reshape(-1, kinds, rows, HD)
    back = jnp.transpose(back, (2, 1, 0, 3)).reshape(rows, -1)
    mixed = jnp.dot(back, w_out_all, preferred_element_type=jnp.float32)
    updated = (inputs + branch_gate * mixed).astype(jnp.bfloat16)
    final = (rms_normalize(updated.astype(jnp.float32)) * final_gain).astype(jnp.bfloat16)
    ids = jnp.broadcast_to(type_ids.astype(jnp.bfloat16), (rows, 128))
    ext = jnp.concatenate([final, ids], axis=1)
    joined = jnp.concatenate([ext] + [shifted(ext, "type", k) for k in range(1, kinds)], axis=0)
    final_all = joined[:, : final.shape[1]]
    kinds_all = joined[:, final.shape[1]].astype(jnp.int32)
    owned = head_w1.shape[0]
    first_kind = lax.axis_index("type") * owned
    result = jnp.zeros((final_all.shape[0], head_w2.shape[2]), jnp.float32)
    for which in range(owned):
        hidden = jnp.dot(final_all, head_w1[which], preferred_element_type=jnp.float32)
        hidden = jax.nn.gelu(hidden + head_b1[which].astype(jnp.float32)).astype(jnp.bfloat16)
        answer = jnp.dot(hidden, head_w2[which], preferred_element_type=jnp.float32)
        result = jnp.where((kinds_all == first_kind + which)[:, None], answer, result)
    result = result.reshape(kinds, rows, -1)
    head_out = result[0]
    for k in range(1, kinds):
        head_out = head_out + shifted(result[(-k) % kinds], "type", k)
    return (updated, head_out)


def solution(mesh):
    seq = mesh.shape["seq"]
    kinds = mesh.shape["type"]
    y_n = 2
    x_n = 4
    z_n = seq // (x_n * y_n)
    split = Mesh(mesh.devices.reshape(z_n, x_n, y_n, kinds), ("z", "x", "y", "type"))
    rows = P(("z", "x", "y", "type"), None)
    in_specs = (
        rows,
        P(),
        P(),
        P(),
        P(None, None, "type"),
        P("type", None),
        rows,
        P("type", None, None),
        P("type", None),
        P("type", None, None),
    )
    out_specs = (rows, rows)
    return jax.shard_map(body, mesh=split, in_specs=in_specs, out_specs=out_specs, check_vma=False)
```

```python
import functools

import jax
import jax.numpy as jnp
from jax import lax
from jax.experimental import pallas as pl
from jax.experimental.pallas import tpu as pltpu
from jax.sharding import Mesh
from jax.sharding import PartitionSpec as P

HD = 64
SCALE = HD ** (-0.5)
QUERY_BLOCK = 544
ROW_SPLIT = 2


def rms_normalize(values):
    squares = jnp.mean(values * values, axis=-1, keepdims=True)
    return values * lax.rsqrt(squares + 1e-06)


def step_kernel(first, last, *refs):
    if first:
        q_ref, kv_ref, out_ref, acc_s = refs
    else:
        q_ref, kv_ref, acc_in, out_ref, acc_s = refs
    chunk = pl.program_id(1)

    @pl.when(chunk == 0)
    def _():
        if first:
            lane = lax.broadcasted_iota(jnp.int32, acc_s.shape, 1)
            acc_s[...] = jnp.where(lane == 1, -jnp.inf, 0.0).astype(jnp.float32)
        else:
            acc_s[...] = acc_in[...]

    kv = kv_ref[...]
    lane = lax.broadcasted_iota(jnp.int32, kv.shape, 1)
    kv_sums = jnp.where(lane < HD, jnp.ones_like(kv), kv)
    rows = q_ref.shape[0] // ROW_SPLIT
    scores = []
    for g in range(ROW_SPLIT):
        scores.append(
            lax.dot_general(
                q_ref[g * rows : (g + 1) * rows, :],
                kv,
                (((1,), (1,)), ((), ())),
                preferred_element_type=jnp.float32,
            )
        )
    for g in range(ROW_SPLIT):
        part = slice(g * rows, (g + 1) * rows)
        held = acc_s[part, :]
        m_old = held[:, 1:2]
        m_new = jnp.maximum(m_old, jnp.max(scores[g], axis=1, keepdims=True))
        decay = jnp.exp(m_old - m_new)
        weights = jnp.exp(scores[g] - m_new).astype(jnp.bfloat16)
        fresh = decay * held + jnp.dot(weights, kv_sums, preferred_element_type=jnp.float32)
        lane_row = lax.broadcasted_iota(jnp.int32, fresh.shape, 1)
        acc_s[part, :] = jnp.where(lane_row == 1, m_new, fresh)

    @pl.when(chunk == pl.num_programs(1) - 1)
    def _():
        if last:
            out_ref[...] = (acc_s[...] / acc_s[:, 0:1]).astype(out_ref.dtype)
        else:
            out_ref[...] = acc_s[...]


def flash_step(q_pad, kv, state, first, last):
    rows, width = q_pad.shape
    chunks, chunk = kv.shape[:2]
    block = QUERY_BLOCK
    row_block = pl.BlockSpec((block, width), lambda i, c: (i, 0))
    in_specs = [row_block, pl.BlockSpec((None, chunk, width), lambda i, c: (c, 0, 0))]
    operands = [q_pad, kv]
    if not first:
        in_specs.append(row_block)
        operands.append(state)
    out_type = jnp.bfloat16 if last else jnp.float32
    return pl.pallas_call(
        functools.partial(step_kernel, first, last),
        grid=(rows // block, chunks),
        in_specs=in_specs,
        out_specs=row_block,
        out_shape=jax.ShapeDtypeStruct((rows, width), out_type),
        scratch_shapes=[pltpu.VMEM((block, width), jnp.float32)],
        compiler_params=pltpu.CompilerParams(dimension_semantics=("arbitrary", "arbitrary")),
        cost_estimate=pl.CostEstimate(
            flops=4 * rows * chunks * chunk * width,
            transcendentals=rows * chunks * chunk,
            bytes_accessed=rows * width * 10 + (rows // block) * chunks * chunk * width * 2,
        ),
    )(*operands)


def shifted(value, axis, k):
    n = lax.axis_size(axis)
    return lax.ppermute(value, axis, [(i, (i + k) % n) for i in range(n)])

def body(
    tokens, shift_scale, branch_gate, final_gain, w_qkv, w_out, type_ids, head_w1, head_b1, head_w2
):
    inputs = tokens.astype(jnp.float32)
    modulated = (rms_normalize(inputs) * (1.0 + shift_scale[1]) + shift_scale[0]).astype(
        jnp.bfloat16
    )
    kinds = lax.axis_size("type")
    gathered = jnp.concatenate(
        [modulated] + [shifted(modulated, "type", k) for k in range(1, kinds)], axis=0
    )
    dim = w_qkv.shape[1]
    local_heads = w_qkv.shape[2] // HD
    parts = w_qkv.reshape(3, dim, local_heads, HD)
    scaled = (parts[0] * SCALE).astype(parts.dtype)
    arranged = jnp.stack([scaled, jnp.zeros_like(scaled), parts[1], parts[2]], axis=2)
    arranged = arranged.reshape(dim, local_heads, 4 * HD)
    arranged = jnp.roll(arranged, -lax.axis_index("x"), axis=1)
    projected = jnp.einsum(
        "rd,dje->jre", gathered, arranged, preferred_element_type=jnp.float32
    ).astype(jnp.bfloat16)
    mine = jnp.concatenate(
        [projected[0]] + [shifted(projected[k], "x", k) for k in range(1, local_heads)], axis=0
    )
    q_pad = mine[:, : 2 * HD]
    chunk = mine[:, 2 * HD :]
    z_n = lax.axis_size("z")
    zr = [(i, (i + 1) % z_n) for i in range(z_n)]
    zl = [(i, (i - 1) % z_n) for i in range(z_n)]
    yy = [(0, 1), (1, 0)]
    held = [chunk]
    state = None
    w_out_all = None
    for stage in range(4):
        if stage == 0:
            following = [
                lax.ppermute(chunk, "z", zr),
                lax.ppermute(chunk, "z", zl),
                lax.ppermute(chunk, "y", yy),
            ]
        elif stage == 1:
            following = [
                lax.ppermute(held[0], "z", zr),
                lax.ppermute(held[2], "z", zr),
                lax.ppermute(held[2], "z", zl),
            ]
        elif stage == 2:
            following = [lax.ppermute(held[1], "z", zr)]
        else:
            following = []
        state = flash_step(q_pad, jnp.stack(held), state, stage == 0, stage == 3)
        if following:
            held, state = lax.optimization_barrier((following, state))
        if stage == 0:
            w_out_dep, held = lax.optimization_barrier((w_out, held))
            w_out_all = lax.all_gather(w_out_dep, "type", axis=0, tiled=True)
    attended = state[:, HD:]
    rows = tokens.shape[0]
    attended = attended.reshape(-1, rows, HD)
    owner = jnp.arange(local_heads * kinds)
    pick = ((lax.axis_index("x") - owner // kinds) % local_heads) * kinds + (
        lax.axis_index("type") - owner % kinds
    ) % kinds
    attended = jnp.take(attended, pick, axis=0)
    back = lax.all_to_all(attended, ("x", "type"), 0, 0, tiled=True)
    back = back.reshape(-1, kinds, rows, HD)
    back = jnp.transpose(back, (2, 1, 0, 3)).reshape(rows, -1)
    mixed = jnp.dot(back, w_out_all, preferred_element_type=jnp.float32)
    updated = (inputs + branch_gate * mixed).astype(jnp.bfloat16)
    final = (rms_normalize(updated.astype(jnp.float32)) * final_gain).astype(jnp.bfloat16)
    ids = jnp.broadcast_to(type_ids.astype(jnp.bfloat16), (rows, 128))
    ext = jnp.concatenate([final, ids], axis=1)
    joined = jnp.concatenate([ext] + [shifted(ext, "type", k) for k in range(1, kinds)], axis=0)
    final_all = joined[:, : final.shape[1]]
    kinds_all = joined[:, final.shape[1]].astype(jnp.int32)
    owned = head_w1.shape[0]
    first_kind = lax.axis_index("type") * owned
    result = jnp.zeros((final_all.shape[0], head_w2.shape[2]), jnp.float32)
    for which in range(owned):
        hidden = jnp.dot(final_all, head_w1[which], preferred_element_type=jnp.float32)
        hidden = jax.nn.gelu(hidden + head_b1[which].astype(jnp.float32)).astype(jnp.bfloat16)
        answer = jnp.dot(hidden, head_w2[which], preferred_element_type=jnp.float32)
        result = jnp.where((kinds_all == first_kind + which)[:, None], answer, result)
    result = result.reshape(kinds, rows, -1)
    head_out = result[0]
    for k in range(1, kinds):
        head_out = head_out + shifted(result[(-k) % kinds], "type", k)
    return (updated, head_out)


def solution(mesh):
    seq = mesh.shape["seq"]
    kinds = mesh.shape["type"]
    y_n = 2
    x_n = 4
    z_n = seq // (x_n * y_n)
    split = Mesh(mesh.devices.reshape(z_n, x_n, y_n, kinds), ("z", "x", "y", "type"))
    rows = P(("z", "x", "y", "type"), None)
    in_specs = (
        rows,
        P(),
        P(),
        P(),
        P(None, None, "type"),
        P("type", None),
        rows,
        P("type", None, None),
        P("type", None),
        P("type", None, None),
    )
    out_specs = (rows, rows)
    return jax.shard_map(body, mesh=split, in_specs=in_specs, out_specs=out_specs, check_vma=False)
```

```python
import functools

import jax
import jax.numpy as jnp
from jax import lax
from jax.experimental import pallas as pl
from jax.experimental.pallas import tpu as pltpu
from jax.sharding import Mesh
from jax.sharding import PartitionSpec as P

HD = 64
SCALE = HD ** (-0.5)
QUERY_BLOCK = 544
ROW_SPLIT = 2


def rms_normalize(values):
    squares = jnp.mean(values * values, axis=-1, keepdims=True)
    return values * lax.rsqrt(squares + 1e-06)


def step_kernel(first, last, *refs):
    if first:
        q_ref, kv_ref, out_ref, acc_s = refs
    else:
        q_ref, kv_ref, acc_in, out_ref, acc_s = refs
    chunk = pl.program_id(1)

    @pl.when(chunk == 0)
    def _():
        if first:
            lane = lax.broadcasted_iota(jnp.int32, acc_s.shape, 1)
            acc_s[...] = jnp.where(lane == 1, -jnp.inf, 0.0).astype(jnp.float32)
        else:
            acc_s[...] = acc_in[...]

    kv = kv_ref[...]
    lane = lax.broadcasted_iota(jnp.int32, kv.shape, 1)
    kv_sums = jnp.where(lane < HD, jnp.ones_like(kv), kv)
    rows = q_ref.shape[0] // ROW_SPLIT
    scores = []
    for g in range(ROW_SPLIT):
        scores.append(
            lax.dot_general(
                q_ref[g * rows : (g + 1) * rows, :],
                kv,
                (((1,), (1,)), ((), ())),
                preferred_element_type=jnp.float32,
            )
        )
    for g in range(ROW_SPLIT):
        part = slice(g * rows, (g + 1) * rows)
        held = acc_s[part, :]
        m_old = held[:, 1:2]
        m_new = jnp.maximum(m_old, jnp.max(scores[g], axis=1, keepdims=True))
        decay = jnp.exp(m_old - m_new)
        weights = jnp.exp(scores[g] - m_new).astype(jnp.bfloat16)
        fresh = decay * held + jnp.dot(weights, kv_sums, preferred_element_type=jnp.float32)
        lane_row = lax.broadcasted_iota(jnp.int32, fresh.shape, 1)
        acc_s[part, :] = jnp.where(lane_row == 1, m_new, fresh)

    @pl.when(chunk == pl.num_programs(1) - 1)
    def _():
        if last:
            out_ref[...] = (acc_s[...] / acc_s[:, 0:1]).astype(out_ref.dtype)
        else:
            out_ref[...] = acc_s[...]


def flash_step(q_pad, kv, state, first, last):
    rows, width = q_pad.shape
    chunks, chunk = kv.shape[:2]
    block = QUERY_BLOCK
    row_block = pl.BlockSpec((block, width), lambda i, c: (i, 0))
    in_specs = [row_block, pl.BlockSpec((None, chunk, width), lambda i, c: (c, 0, 0))]
    operands = [q_pad, kv]
    if not first:
        in_specs.append(row_block)
        operands.append(state)
    out_type = jnp.bfloat16 if last else jnp.float32
    return pl.pallas_call(
        functools.partial(step_kernel, first, last),
        grid=(rows // block, chunks),
        in_specs=in_specs,
        out_specs=row_block,
        out_shape=jax.ShapeDtypeStruct((rows, width), out_type),
        scratch_shapes=[pltpu.VMEM((block, width), jnp.float32)],
        compiler_params=pltpu.CompilerParams(dimension_semantics=("arbitrary", "arbitrary")),
        cost_estimate=pl.CostEstimate(
            flops=4 * rows * chunks * chunk * width,
            transcendentals=rows * chunks * chunk,
            bytes_accessed=rows * width * 10 + (rows // block) * chunks * chunk * width * 2,
        ),
    )(*operands)


def shifted(value, axis, k):
    n = lax.axis_size(axis)
    return lax.ppermute(value, axis, [(i, (i + k) % n) for i in range(n)])

def body(
    tokens, shift_scale, branch_gate, final_gain, w_qkv, w_out, type_ids, head_w1, head_b1, head_w2
):
    inputs = tokens.astype(jnp.float32)
    modulated = (rms_normalize(inputs) * (1.0 + shift_scale[1]) + shift_scale[0]).astype(
        jnp.bfloat16
    )
    kinds = lax.axis_size("type")
    gathered = jnp.concatenate(
        [modulated] + [shifted(modulated, "type", k) for k in range(1, kinds)], axis=0
    )
    dim = w_qkv.shape[1]
    local_heads = w_qkv.shape[2] // HD
    parts = w_qkv.reshape(3, dim, local_heads, HD)
    scaled = (parts[0] * SCALE).astype(parts.dtype)
    arranged = jnp.stack([scaled, jnp.zeros_like(scaled), parts[1], parts[2]], axis=2)
    arranged = arranged.reshape(dim, local_heads, 4 * HD)
    arranged = jnp.roll(arranged, -lax.axis_index("x"), axis=1)
    projected = jnp.einsum(
        "rd,dje->jre", gathered, arranged, preferred_element_type=jnp.float32
    ).astype(jnp.bfloat16)
    mine = jnp.concatenate(
        [projected[0]] + [shifted(projected[k], "x", k) for k in range(1, local_heads)], axis=0
    )
    q_pad = mine[:, : 2 * HD]
    chunk = mine[:, 2 * HD :]
    z_n = lax.axis_size("z")
    zr = [(i, (i + 1) % z_n) for i in range(z_n)]
    zl = [(i, (i - 1) % z_n) for i in range(z_n)]
    yy = [(0, 1), (1, 0)]
    held = [chunk]
    state = None
    w_out_all = None
    for stage in range(4):
        if stage == 0:
            following = [
                lax.ppermute(chunk, "z", zr),
                lax.ppermute(chunk, "z", zl),
                lax.ppermute(chunk, "y", yy),
            ]
        elif stage == 1:
            following = [
                lax.ppermute(held[0], "z", zr),
                lax.ppermute(held[2], "z", zr),
                lax.ppermute(held[2], "z", zl),
            ]
        elif stage == 2:
            following = [lax.ppermute(held[1], "z", zr)]
        else:
            following = []
        state = flash_step(q_pad, jnp.stack(held), state, stage == 0, stage == 3)
        if following:
            held, state = lax.optimization_barrier((following, state))
        if stage == 0:
            w_out_dep, held = lax.optimization_barrier((w_out, held))
            w_out_all = lax.all_gather(w_out_dep, "type", axis=0, tiled=True)
    attended = state[:, HD:]
    rows = tokens.shape[0]
    attended = attended.reshape(-1, rows, HD)
    owner = jnp.arange(local_heads * kinds)
    pick = ((lax.axis_index("x") - owner // kinds) % local_heads) * kinds + (
        lax.axis_index("type") - owner % kinds
    ) % kinds
    attended = jnp.take(attended, pick, axis=0)
    back = lax.all_to_all(attended, ("x", "type"), 0, 0, tiled=True)
    back = back.reshape(-1, kinds, rows, HD)
    back = jnp.transpose(back, (2, 1, 0, 3)).reshape(rows, -1)
    mixed = jnp.dot(back, w_out_all, preferred_element_type=jnp.float32)
    updated = (inputs + branch_gate * mixed).astype(jnp.bfloat16)
    final = (rms_normalize(updated.astype(jnp.float32)) * final_gain).astype(jnp.bfloat16)
    ids = jnp.broadcast_to(type_ids.astype(jnp.bfloat16), (rows, 128))
    ext = jnp.concatenate([final, ids], axis=1)
    owned = head_w1.shape[0]
    first_kind = lax.axis_index("type") * owned

    def heads_of(block):
        features = block[:, : final.shape[1]]
        block_kinds = block[:, final.shape[1]].astype(jnp.int32)
        result = jnp.zeros((rows, head_w2.shape[2]), jnp.float32)
        for which in range(owned):
            hidden = jnp.dot(features, head_w1[which], preferred_element_type=jnp.float32)
            hidden = jax.nn.gelu(hidden + head_b1[which].astype(jnp.float32)).astype(jnp.bfloat16)
            answer = jnp.dot(hidden, head_w2[which], preferred_element_type=jnp.float32)
            result = jnp.where((block_kinds == first_kind + which)[:, None], answer, result)
        return result

    arriving = [shifted(ext, "type", k) for k in range(1, kinds)]
    head_out = heads_of(ext)
    for k in range(1, kinds):
        head_out = head_out + shifted(heads_of(arriving[k - 1]), "type", -k)
    return (updated, head_out)


def solution(mesh):
    seq = mesh.shape["seq"]
    kinds = mesh.shape["type"]
    y_n = 2
    x_n = 4
    z_n = seq // (x_n * y_n)
    split = Mesh(mesh.devices.reshape(z_n, x_n, y_n, kinds), ("z", "x", "y", "type"))
    rows = P(("z", "x", "y", "type"), None)
    in_specs = (
        rows,
        P(),
        P(),
        P(),
        P(None, None, "type"),
        P("type", None),
        rows,
        P("type", None, None),
        P("type", None),
        P("type", None, None),
    )
    out_specs = (rows, rows)
    return jax.shard_map(body, mesh=split, in_specs=in_specs, out_specs=out_specs, check_vma=False)
```

```python
import functools

import jax
import jax.numpy as jnp
from jax import lax
from jax.experimental import pallas as pl
from jax.experimental.pallas import tpu as pltpu
from jax.sharding import Mesh
from jax.sharding import PartitionSpec as P

HD = 64
SCALE = HD ** (-0.5)
QUERY_BLOCK = 1088
ROW_SPLIT = 2


def rms_normalize(values):
    squares = jnp.mean(values * values, axis=-1, keepdims=True)
    return values * lax.rsqrt(squares + 1e-06)


def step_kernel(first, last, *refs):
    if first:
        q_ref, kv_ref, out_ref, acc_s = refs
    else:
        q_ref, kv_ref, acc_in, out_ref, acc_s = refs
    chunk = pl.program_id(1)

    @pl.when(chunk == 0)
    def _():
        if first:
            lane = lax.broadcasted_iota(jnp.int32, acc_s.shape, 1)
            acc_s[...] = jnp.where(lane == 1, -jnp.inf, 0.0).astype(jnp.float32)
        else:
            acc_s[...] = acc_in[...]

    kv = kv_ref[...]
    lane = lax.broadcasted_iota(jnp.int32, kv.shape, 1)
    kv_sums = jnp.where(lane < HD, jnp.ones_like(kv), kv)
    rows = q_ref.shape[0] // ROW_SPLIT
    scores = []
    for g in range(ROW_SPLIT):
        scores.append(
            lax.dot_general(
                q_ref[g * rows : (g + 1) * rows, :],
                kv,
                (((1,), (1,)), ((), ())),
                preferred_element_type=jnp.float32,
            )
        )
    for g in range(ROW_SPLIT):
        part = slice(g * rows, (g + 1) * rows)
        held = acc_s[part, :]
        m_old = held[:, 1:2]
        m_new = jnp.maximum(m_old, jnp.max(scores[g], axis=1, keepdims=True))
        decay = jnp.exp(m_old - m_new)
        weights = jnp.exp(scores[g] - m_new).astype(jnp.bfloat16)
        fresh = decay * held + jnp.dot(weights, kv_sums, preferred_element_type=jnp.float32)
        lane_row = lax.broadcasted_iota(jnp.int32, fresh.shape, 1)
        acc_s[part, :] = jnp.where(lane_row == 1, m_new, fresh)

    @pl.when(chunk == pl.num_programs(1) - 1)
    def _():
        if last:
            out_ref[...] = (acc_s[...] / acc_s[:, 0:1]).astype(out_ref.dtype)
        else:
            out_ref[...] = acc_s[...]


def flash_step(q_pad, kv, state, first, last):
    rows, width = q_pad.shape
    chunks, chunk = kv.shape[:2]
    block = QUERY_BLOCK
    row_block = pl.BlockSpec((block, width), lambda i, c: (i, 0))
    in_specs = [row_block, pl.BlockSpec((None, chunk, width), lambda i, c: (c, 0, 0))]
    operands = [q_pad, kv]
    if not first:
        in_specs.append(row_block)
        operands.append(state)
    out_type = jnp.bfloat16 if last else jnp.float32
    return pl.pallas_call(
        functools.partial(step_kernel, first, last),
        grid=(rows // block, chunks),
        in_specs=in_specs,
        out_specs=row_block,
        out_shape=jax.ShapeDtypeStruct((rows, width), out_type),
        scratch_shapes=[pltpu.VMEM((block, width), jnp.float32)],
        compiler_params=pltpu.CompilerParams(dimension_semantics=("arbitrary", "arbitrary")),
        cost_estimate=pl.CostEstimate(
            flops=4 * rows * chunks * chunk * width,
            transcendentals=rows * chunks * chunk,
            bytes_accessed=rows * width * 10 + (rows // block) * chunks * chunk * width * 2,
        ),
    )(*operands)


def shifted(value, axis, k):
    n = lax.axis_size(axis)
    return lax.ppermute(value, axis, [(i, (i + k) % n) for i in range(n)])

def body(
    tokens, shift_scale, branch_gate, final_gain, w_qkv, w_out, type_ids, head_w1, head_b1, head_w2
):
    inputs = tokens.astype(jnp.float32)
    modulated = (rms_normalize(inputs) * (1.0 + shift_scale[1]) + shift_scale[0]).astype(
        jnp.bfloat16
    )
    kinds = lax.axis_size("type")
    gathered = jnp.concatenate(
        [modulated] + [shifted(modulated, "type", k) for k in range(1, kinds)], axis=0
    )
    dim = w_qkv.shape[1]
    local_heads = w_qkv.shape[2] // HD
    parts = w_qkv.reshape(3, dim, local_heads, HD)
    scaled = (parts[0] * SCALE).astype(parts.dtype)
    arranged = jnp.stack([scaled, jnp.zeros_like(scaled), parts[1], parts[2]], axis=2)
    arranged = arranged.reshape(dim, local_heads, 4 * HD)
    arranged = jnp.roll(arranged, -lax.axis_index("x"), axis=1)
    projected = jnp.einsum(
        "rd,dje->jre", gathered, arranged, preferred_element_type=jnp.float32
    ).astype(jnp.bfloat16)
    mine = jnp.concatenate(
        [projected[0]] + [shifted(projected[k], "x", k) for k in range(1, local_heads)], axis=0
    )
    q_pad = mine[:, : 2 * HD]
    chunk = mine[:, 2 * HD :]
    z_n = lax.axis_size("z")
    zr = [(i, (i + 1) % z_n) for i in range(z_n)]
    zl = [(i, (i - 1) % z_n) for i in range(z_n)]
    yy = [(0, 1), (1, 0)]
    held = [chunk]
    state = None
    w_out_all = None
    for stage in range(4):
        if stage == 0:
            following = [
                lax.ppermute(chunk, "z", zr),
                lax.ppermute(chunk, "z", zl),
                lax.ppermute(chunk, "y", yy),
            ]
        elif stage == 1:
            following = [
                lax.ppermute(held[0], "z", zr),
                lax.ppermute(held[2], "z", zr),
                lax.ppermute(held[2], "z", zl),
            ]
        elif stage == 2:
            following = [lax.ppermute(held[1], "z", zr)]
        else:
            following = []
        state = flash_step(q_pad, jnp.stack(held), state, stage == 0, stage == 3)
        if following:
            held, state = lax.optimization_barrier((following, state))
        if stage == 0:
            w_out_dep, held = lax.optimization_barrier((w_out, held))
            w_out_all = lax.all_gather(w_out_dep, "type", axis=0, tiled=True)
    attended = state[:, HD:]
    rows = tokens.shape[0]
    attended = attended.reshape(-1, rows, HD)
    owner = jnp.arange(local_heads * kinds)
    pick = ((lax.axis_index("x") - owner // kinds) % local_heads) * kinds + (
        lax.axis_index("type") - owner % kinds
    ) % kinds
    attended = jnp.take(attended, pick, axis=0)
    back = lax.all_to_all(attended, ("x", "type"), 0, 0, tiled=True)
    back = back.reshape(-1, kinds, rows, HD)
    back = jnp.transpose(back, (2, 1, 0, 3)).reshape(rows, -1)
    mixed = jnp.dot(back, w_out_all, preferred_element_type=jnp.float32)
    updated = (inputs + branch_gate * mixed).astype(jnp.bfloat16)
    final = (rms_normalize(updated.astype(jnp.float32)) * final_gain).astype(jnp.bfloat16)
    ids = jnp.broadcast_to(type_ids.astype(jnp.bfloat16), (rows, 128))
    ext = jnp.concatenate([final, ids], axis=1)
    joined = jnp.concatenate([ext] + [shifted(ext, "type", k) for k in range(1, kinds)], axis=0)
    final_all = joined[:, : final.shape[1]]
    kinds_all = joined[:, final.shape[1]].astype(jnp.int32)
    owned = head_w1.shape[0]
    first_kind = lax.axis_index("type") * owned
    result = jnp.zeros((final_all.shape[0], head_w2.shape[2]), jnp.float32)
    for which in range(owned):
        hidden = jnp.dot(final_all, head_w1[which], preferred_element_type=jnp.float32)
        hidden = jax.nn.gelu(hidden + head_b1[which].astype(jnp.float32)).astype(jnp.bfloat16)
        answer = jnp.dot(hidden, head_w2[which], preferred_element_type=jnp.float32)
        result = jnp.where((kinds_all == first_kind + which)[:, None], answer, result)
    result = result.reshape(kinds, rows, -1)
    head_out = result[0]
    for k in range(1, kinds):
        head_out = head_out + shifted(result[(-k) % kinds], "type", k)
    return (updated, head_out)


def solution(mesh):
    seq = mesh.shape["seq"]
    kinds = mesh.shape["type"]
    y_n = 2
    x_n = 4
    z_n = seq // (x_n * y_n)
    split = Mesh(mesh.devices.reshape(z_n, x_n, y_n, kinds), ("z", "x", "y", "type"))
    rows = P(("z", "x", "y", "type"), None)
    in_specs = (
        rows,
        P(),
        P(),
        P(),
        P(None, None, "type"),
        P("type", None),
        rows,
        P("type", None, None),
        P("type", None),
        P("type", None, None),
    )
    out_specs = (rows, rows)
    return jax.shard_map(body, mesh=split, in_specs=in_specs, out_specs=out_specs, check_vma=False)
```

```python
import functools

import jax
import jax.numpy as jnp
from jax import lax
from jax.experimental import pallas as pl
from jax.experimental.pallas import tpu as pltpu
from jax.sharding import Mesh
from jax.sharding import PartitionSpec as P

HD = 64
SCALE = HD ** (-0.5)
QUERY_BLOCK = 1088
ROW_SPLIT = 2


def rms_normalize(values):
    squares = jnp.mean(values * values, axis=-1, keepdims=True)
    return values * lax.rsqrt(squares + 1e-06)


def step_kernel(first, last, *refs):
    if first:
        q_ref, kv_ref, out_ref, acc_s = refs
    else:
        q_ref, kv_ref, acc_in, out_ref, acc_s = refs
    chunk = pl.program_id(1)

    @pl.when(chunk == 0)
    def _():
        if first:
            lane = lax.broadcasted_iota(jnp.int32, acc_s.shape, 1)
            acc_s[...] = jnp.where(lane == 1, -jnp.inf, 0.0).astype(jnp.float32)
        else:
            acc_s[...] = acc_in[...]

    kv = kv_ref[...]
    lane = lax.broadcasted_iota(jnp.int32, kv.shape, 1)
    kv_sums = jnp.where(lane < HD, jnp.ones_like(kv), kv)
    rows = q_ref.shape[0] // ROW_SPLIT
    scores = []
    for g in range(ROW_SPLIT):
        scores.append(
            lax.dot_general(
                q_ref[g * rows : (g + 1) * rows, :],
                kv,
                (((1,), (1,)), ((), ())),
                preferred_element_type=jnp.float32,
            )
        )
    for g in range(ROW_SPLIT):
        part = slice(g * rows, (g + 1) * rows)
        held = acc_s[part, :]
        m_old = held[:, 1:2]
        m_new = jnp.maximum(m_old, jnp.max(scores[g], axis=1, keepdims=True))
        decay = jnp.exp(m_old - m_new)
        weights = jnp.exp(scores[g] - m_new).astype(jnp.bfloat16)
        fresh = decay * held + jnp.dot(weights, kv_sums, preferred_element_type=jnp.float32)
        lane_row = lax.broadcasted_iota(jnp.int32, fresh.shape, 1)
        acc_s[part, :] = jnp.where(lane_row == 1, m_new, fresh)

    @pl.when(chunk == pl.num_programs(1) - 1)
    def _():
        if last:
            out_ref[...] = (acc_s[...] / acc_s[:, 0:1]).astype(out_ref.dtype)
        else:
            out_ref[...] = acc_s[...]


def flash_step(q_pad, kv, state, first, last):
    rows, width = q_pad.shape
    chunks, chunk = kv.shape[:2]
    block = QUERY_BLOCK
    row_block = pl.BlockSpec((block, width), lambda i, c: (i, 0))
    in_specs = [row_block, pl.BlockSpec((None, chunk, width), lambda i, c: (c, 0, 0))]
    operands = [q_pad, kv]
    if not first:
        in_specs.append(row_block)
        operands.append(state)
    out_type = jnp.bfloat16 if last else jnp.float32
    return pl.pallas_call(
        functools.partial(step_kernel, first, last),
        grid=(rows // block, chunks),
        in_specs=in_specs,
        out_specs=row_block,
        out_shape=jax.ShapeDtypeStruct((rows, width), out_type),
        scratch_shapes=[pltpu.VMEM((block, width), jnp.float32)],
        compiler_params=pltpu.CompilerParams(dimension_semantics=("arbitrary", "arbitrary")),
        cost_estimate=pl.CostEstimate(
            flops=4 * rows * chunks * chunk * width,
            transcendentals=rows * chunks * chunk,
            bytes_accessed=rows * width * 10 + (rows // block) * chunks * chunk * width * 2,
        ),
    )(*operands)


def shifted(value, axis, k):
    n = lax.axis_size(axis)
    return lax.ppermute(value, axis, [(i, (i + k) % n) for i in range(n)])

def body(
    tokens, shift_scale, branch_gate, final_gain, w_qkv, w_out, type_ids, head_w1, head_b1, head_w2
):
    inputs = tokens.astype(jnp.float32)
    modulated = (rms_normalize(inputs) * (1.0 + shift_scale[1]) + shift_scale[0]).astype(
        jnp.bfloat16
    )
    kinds = lax.axis_size("type")
    gathered = jnp.concatenate(
        [modulated] + [shifted(modulated, "type", k) for k in range(1, kinds)], axis=0
    )
    dim = w_qkv.shape[1]
    local_heads = w_qkv.shape[2] // HD
    parts = w_qkv.reshape(3, dim, local_heads, HD)
    scaled = (parts[0] * SCALE).astype(parts.dtype)
    arranged = jnp.stack([scaled, jnp.zeros_like(scaled), parts[1], parts[2]], axis=2)
    arranged = arranged.reshape(dim, local_heads, 4 * HD)
    arranged = jnp.roll(arranged, -lax.axis_index("x"), axis=1)
    projected = jnp.einsum(
        "rd,dje->jre", gathered, arranged, preferred_element_type=jnp.float32
    ).astype(jnp.bfloat16)
    mine = jnp.concatenate(
        [projected[0]] + [shifted(projected[k], "x", k) for k in range(1, local_heads)], axis=0
    )
    q_pad = mine[:, : 2 * HD]
    chunk = mine[:, 2 * HD :]
    z_n = lax.axis_size("z")
    zr = [(i, (i + 1) % z_n) for i in range(z_n)]
    zl = [(i, (i - 1) % z_n) for i in range(z_n)]
    yy = [(0, 1), (1, 0)]
    held = [chunk]
    state = None
    w_out_all = None
    for stage in range(4):
        if stage == 0:
            following = [
                lax.ppermute(chunk, "z", zr),
                lax.ppermute(chunk, "z", zl),
                lax.ppermute(chunk, "y", yy),
            ]
        elif stage == 1:
            following = [
                lax.ppermute(held[0], "z", zr),
                lax.ppermute(held[2], "z", zr),
                lax.ppermute(held[2], "z", zl),
            ]
        elif stage == 2:
            following = [lax.ppermute(held[1], "z", zr)]
        else:
            following = []
        state = flash_step(q_pad, jnp.stack(held), state, stage == 0, stage == 3)
        if following:
            held, state = lax.optimization_barrier((following, state))
        if stage == 0:
            w_out_dep, held = lax.optimization_barrier((w_out, held))
            w_out_all = lax.all_gather(w_out_dep, "type", axis=0, tiled=True)
    attended = state[:, HD:]
    rows = tokens.shape[0]
    attended = attended.reshape(-1, rows, HD)
    owner = jnp.arange(local_heads * kinds)
    pick = ((lax.axis_index("x") - owner // kinds) % local_heads) * kinds + (
        lax.axis_index("type") - owner % kinds
    ) % kinds
    attended = jnp.take(attended, pick, axis=0)
    back = lax.all_to_all(attended, ("x", "type"), 0, 0, tiled=True)
    back = back.reshape(-1, kinds, rows, HD)
    back = jnp.transpose(back, (2, 1, 0, 3)).reshape(rows, -1)
    mixed = jnp.dot(back, w_out_all, preferred_element_type=jnp.float32)
    updated = (inputs + branch_gate * mixed).astype(jnp.bfloat16)
    final = (rms_normalize(updated.astype(jnp.float32)) * final_gain).astype(jnp.bfloat16)
    ids = jnp.broadcast_to(type_ids.astype(jnp.bfloat16), (rows, 128))
    ext = jnp.concatenate([final, ids], axis=1)
    owned = head_w1.shape[0]
    first_kind = lax.axis_index("type") * owned

    def heads_of(block):
        features = block[:, : final.shape[1]]
        block_kinds = block[:, final.shape[1]].astype(jnp.int32)
        result = jnp.zeros((block.shape[0], head_w2.shape[2]), jnp.float32)
        for which in range(owned):
            hidden = jnp.dot(features, head_w1[which], preferred_element_type=jnp.float32)
            hidden = jax.nn.gelu(hidden + head_b1[which].astype(jnp.float32)).astype(jnp.bfloat16)
            answer = jnp.dot(hidden, head_w2[which], preferred_element_type=jnp.float32)
            result = jnp.where((block_kinds == first_kind + which)[:, None], answer, result)
        return result

    arriving = jnp.concatenate([shifted(ext, "type", k) for k in range(1, kinds)], axis=0)
    head_out = heads_of(ext)
    others = heads_of(arriving).reshape(kinds - 1, rows, -1)
    for k in range(1, kinds):
        head_out = head_out + shifted(others[k - 1], "type", -k)
    return (updated, head_out)


def solution(mesh):
    seq = mesh.shape["seq"]
    kinds = mesh.shape["type"]
    y_n = 2
    x_n = 4
    z_n = seq // (x_n * y_n)
    split = Mesh(mesh.devices.reshape(z_n, x_n, y_n, kinds), ("z", "x", "y", "type"))
    rows = P(("z", "x", "y", "type"), None)
    in_specs = (
        rows,
        P(),
        P(),
        P(),
        P(None, None, "type"),
        P("type", None),
        rows,
        P("type", None, None),
        P("type", None),
        P("type", None, None),
    )
    out_specs = (rows, rows)
    return jax.shard_map(body, mesh=split, in_specs=in_specs, out_specs=out_specs, check_vma=False)
```

```python
import functools

import jax
import jax.numpy as jnp
from jax import lax
from jax.experimental import pallas as pl
from jax.experimental.pallas import tpu as pltpu
from jax.sharding import Mesh
from jax.sharding import PartitionSpec as P

HD = 64
SCALE = HD ** (-0.5)
QUERY_BLOCK = 1088
ROW_SPLIT = 2


def rms_normalize(values):
    squares = jnp.mean(values * values, axis=-1, keepdims=True)
    return values * lax.rsqrt(squares + 1e-06)


def step_kernel(first, last, *refs):
    if first:
        q_ref, kv_ref, out_ref, acc_s = refs
    else:
        q_ref, kv_ref, acc_in, out_ref, acc_s = refs
    chunk = pl.program_id(1)

    @pl.when(chunk == 0)
    def _():
        if first:
            lane = lax.broadcasted_iota(jnp.int32, acc_s.shape, 1)
            acc_s[...] = jnp.where(lane == 1, -jnp.inf, 0.0).astype(jnp.float32)
        else:
            acc_s[...] = acc_in[...]

    kv = kv_ref[...]
    lane = lax.broadcasted_iota(jnp.int32, kv.shape, 1)
    kv_sums = jnp.where(lane < HD, jnp.ones_like(kv), kv)
    rows = q_ref.shape[0] // ROW_SPLIT
    scores = []
    for g in range(ROW_SPLIT):
        scores.append(
            lax.dot_general(
                q_ref[g * rows : (g + 1) * rows, :],
                kv,
                (((1,), (1,)), ((), ())),
                preferred_element_type=jnp.float32,
            )
        )
    for g in range(ROW_SPLIT):
        part = slice(g * rows, (g + 1) * rows)
        held = acc_s[part, :]
        m_old = held[:, 1:2]
        m_new = jnp.maximum(m_old, jnp.max(scores[g], axis=1, keepdims=True))
        decay = jnp.exp(m_old - m_new)
        weights = jnp.exp(scores[g] - m_new).astype(jnp.bfloat16)
        fresh = decay * held + jnp.dot(weights, kv_sums, preferred_element_type=jnp.float32)
        lane_row = lax.broadcasted_iota(jnp.int32, fresh.shape, 1)
        acc_s[part, :] = jnp.where(lane_row == 1, m_new, fresh)

    @pl.when(chunk == pl.num_programs(1) - 1)
    def _():
        if last:
            out_ref[...] = (acc_s[:, HD:] / acc_s[:, 0:1]).astype(out_ref.dtype)
        else:
            out_ref[...] = acc_s[...]


def flash_step(q_pad, kv, state, first, last):
    rows, width = q_pad.shape
    chunks, chunk = kv.shape[:2]
    block = QUERY_BLOCK
    row_block = pl.BlockSpec((block, width), lambda i, c: (i, 0))
    in_specs = [row_block, pl.BlockSpec((None, chunk, width), lambda i, c: (c, 0, 0))]
    operands = [q_pad, kv]
    if not first:
        in_specs.append(row_block)
        operands.append(state)
    if last:
        out_specs = pl.BlockSpec((block, HD), lambda i, c: (i, 0))
        out_shape = jax.ShapeDtypeStruct((rows, HD), jnp.bfloat16)
    else:
        out_specs = row_block
        out_shape = jax.ShapeDtypeStruct((rows, width), jnp.float32)
    return pl.pallas_call(
        functools.partial(step_kernel, first, last),
        grid=(rows // block, chunks),
        in_specs=in_specs,
        out_specs=out_specs,
        out_shape=out_shape,
        scratch_shapes=[pltpu.VMEM((block, width), jnp.float32)],
        compiler_params=pltpu.CompilerParams(dimension_semantics=("arbitrary", "arbitrary")),
        cost_estimate=pl.CostEstimate(
            flops=4 * rows * chunks * chunk * width,
            transcendentals=rows * chunks * chunk,
            bytes_accessed=rows * width * 10 + (rows // block) * chunks * chunk * width * 2,
        ),
    )(*operands)


def shifted(value, axis, k):
    n = lax.axis_size(axis)
    return lax.ppermute(value, axis, [(i, (i + k) % n) for i in range(n)])

def body(
    tokens, shift_scale, branch_gate, final_gain, w_qkv, w_out, type_ids, head_w1, head_b1, head_w2
):
    inputs = tokens.astype(jnp.float32)
    modulated = (rms_normalize(inputs) * (1.0 + shift_scale[1]) + shift_scale[0]).astype(
        jnp.bfloat16
    )
    kinds = lax.axis_size("type")
    gathered = jnp.concatenate(
        [modulated] + [shifted(modulated, "type", k) for k in range(1, kinds)], axis=0
    )
    dim = w_qkv.shape[1]
    local_heads = w_qkv.shape[2] // HD
    parts = w_qkv.reshape(3, dim, local_heads, HD)
    scaled = (parts[0] * SCALE).astype(parts.dtype)
    arranged = jnp.stack([scaled, jnp.zeros_like(scaled), parts[1], parts[2]], axis=2)
    arranged = arranged.reshape(dim, local_heads, 4 * HD)
    arranged = jnp.roll(arranged, -lax.axis_index("x"), axis=1)
    projected = jnp.einsum(
        "rd,dje->jre", gathered, arranged, preferred_element_type=jnp.float32
    ).astype(jnp.bfloat16)
    mine = jnp.concatenate(
        [projected[0]] + [shifted(projected[k], "x", k) for k in range(1, local_heads)], axis=0
    )
    q_pad = mine[:, : 2 * HD]
    chunk = mine[:, 2 * HD :]
    z_n = lax.axis_size("z")
    zr = [(i, (i + 1) % z_n) for i in range(z_n)]
    zl = [(i, (i - 1) % z_n) for i in range(z_n)]
    yy = [(0, 1), (1, 0)]
    held = [chunk]
    state = None
    w_out_all = None
    for stage in range(4):
        if stage == 0:
            following = [
                lax.ppermute(chunk, "z", zr),
                lax.ppermute(chunk, "z", zl),
                lax.ppermute(chunk, "y", yy),
            ]
        elif stage == 1:
            following = [
                lax.ppermute(held[0], "z", zr),
                lax.ppermute(held[2], "z", zr),
                lax.ppermute(held[2], "z", zl),
            ]
        elif stage == 2:
            following = [lax.ppermute(held[1], "z", zr)]
        else:
            following = []
        state = flash_step(q_pad, jnp.stack(held), state, stage == 0, stage == 3)
        if following:
            held, state = lax.optimization_barrier((following, state))
        if stage == 0:
            w_out_dep, held = lax.optimization_barrier((w_out, held))
            w_out_all = lax.all_gather(w_out_dep, "type", axis=0, tiled=True)
    attended = state
    rows = tokens.shape[0]
    attended = attended.reshape(-1, rows, HD)
    owner = jnp.arange(local_heads * kinds)
    pick = ((lax.axis_index("x") - owner // kinds) % local_heads) * kinds + (
        lax.axis_index("type") - owner % kinds
    ) % kinds
    attended = jnp.take(attended, pick, axis=0)
    back = lax.all_to_all(attended, ("x", "type"), 0, 0, tiled=True)
    back = back.reshape(-1, kinds, rows, HD)
    back = jnp.transpose(back, (2, 1, 0, 3)).reshape(rows, -1)
    mixed = jnp.dot(back, w_out_all, preferred_element_type=jnp.float32)
    updated = (inputs + branch_gate * mixed).astype(jnp.bfloat16)
    final = (rms_normalize(updated.astype(jnp.float32)) * final_gain).astype(jnp.bfloat16)
    ids = jnp.broadcast_to(type_ids.astype(jnp.bfloat16), (rows, 128))
    ext = jnp.concatenate([final, ids], axis=1)
    joined = jnp.concatenate([ext] + [shifted(ext, "type", k) for k in range(1, kinds)], axis=0)
    final_all = joined[:, : final.shape[1]]
    kinds_all = joined[:, final.shape[1]].astype(jnp.int32)
    owned = head_w1.shape[0]
    first_kind = lax.axis_index("type") * owned
    result = jnp.zeros((final_all.shape[0], head_w2.shape[2]), jnp.float32)
    for which in range(owned):
        hidden = jnp.dot(final_all, head_w1[which], preferred_element_type=jnp.float32)
        hidden = jax.nn.gelu(hidden + head_b1[which].astype(jnp.float32)).astype(jnp.bfloat16)
        answer = jnp.dot(hidden, head_w2[which], preferred_element_type=jnp.float32)
        result = jnp.where((kinds_all == first_kind + which)[:, None], answer, result)
    result = result.reshape(kinds, rows, -1)
    head_out = result[0]
    for k in range(1, kinds):
        head_out = head_out + shifted(result[(-k) % kinds], "type", k)
    return (updated, head_out)


def solution(mesh):
    seq = mesh.shape["seq"]
    kinds = mesh.shape["type"]
    y_n = 2
    x_n = 4
    z_n = seq // (x_n * y_n)
    split = Mesh(mesh.devices.reshape(z_n, x_n, y_n, kinds), ("z", "x", "y", "type"))
    rows = P(("z", "x", "y", "type"), None)
    in_specs = (
        rows,
        P(),
        P(),
        P(),
        P(None, None, "type"),
        P("type", None),
        rows,
        P("type", None, None),
        P("type", None),
        P("type", None, None),
    )
    out_specs = (rows, rows)
    return jax.shard_map(body, mesh=split, in_specs=in_specs, out_specs=out_specs, check_vma=False)
```

```python
import functools

import jax
import jax.numpy as jnp
from jax import lax
from jax.experimental import pallas as pl
from jax.experimental.pallas import tpu as pltpu
from jax.sharding import Mesh
from jax.sharding import PartitionSpec as P

HD = 64
SCALE = HD ** (-0.5)
QUERY_BLOCK = 1088
ROW_SPLIT = 2


def rms_normalize(values):
    squares = jnp.mean(values * values, axis=-1, keepdims=True)
    return values * lax.rsqrt(squares + 1e-06)


def step_kernel(first, last, *refs):
    if first:
        q_ref, kv_ref, out_ref, acc_s = refs
    else:
        q_ref, kv_ref, acc_in, out_ref, acc_s = refs
    chunk = pl.program_id(1)

    @pl.when(chunk == 0)
    def _():
        if first:
            lane = lax.broadcasted_iota(jnp.int32, acc_s.shape, 1)
            acc_s[...] = jnp.where(lane == 1, -jnp.inf, 0.0).astype(jnp.float32)
        else:
            acc_s[...] = acc_in[...]

    kv = kv_ref[...]
    lane = lax.broadcasted_iota(jnp.int32, kv.shape, 1)
    kv_sums = jnp.where(lane < HD, jnp.ones_like(kv), kv)
    rows = q_ref.shape[0] // ROW_SPLIT
    scores = []
    for g in range(ROW_SPLIT):
        scores.append(
            lax.dot_general(
                q_ref[g * rows : (g + 1) * rows, :],
                kv,
                (((1,), (1,)), ((), ())),
                preferred_element_type=jnp.float32,
            )
        )
    for g in range(ROW_SPLIT):
        part = slice(g * rows, (g + 1) * rows)
        held = acc_s[part, :]
        m_old = held[:, 1:2]
        m_new = jnp.maximum(m_old, jnp.max(scores[g], axis=1, keepdims=True))
        decay = jnp.exp(m_old - m_new)
        weights = jnp.exp(scores[g] - m_new).astype(jnp.bfloat16)
        fresh = decay * held + jnp.dot(weights, kv_sums, preferred_element_type=jnp.float32)
        lane_row = lax.broadcasted_iota(jnp.int32, fresh.shape, 1)
        acc_s[part, :] = jnp.where(lane_row == 1, m_new, fresh)

    @pl.when(chunk == pl.num_programs(1) - 1)
    def _():
        if last:
            out_ref[...] = (acc_s[...] / acc_s[:, 0:1]).astype(out_ref.dtype)
        else:
            out_ref[...] = acc_s[...]


def flash_step(q_pad, kv, state, first, last):
    rows, width = q_pad.shape
    chunks, chunk = kv.shape[:2]
    block = QUERY_BLOCK
    row_block = pl.BlockSpec((block, width), lambda i, c: (i, 0))
    in_specs = [row_block, pl.BlockSpec((None, chunk, width), lambda i, c: (c, 0, 0))]
    operands = [q_pad, kv]
    if not first:
        in_specs.append(row_block)
        operands.append(state)
    out_type = jnp.bfloat16 if last else jnp.float32
    return pl.pallas_call(
        functools.partial(step_kernel, first, last),
        grid=(rows // block, chunks),
        in_specs=in_specs,
        out_specs=row_block,
        out_shape=jax.ShapeDtypeStruct((rows, width), out_type),
        scratch_shapes=[pltpu.VMEM((block, width), jnp.float32)],
        compiler_params=pltpu.CompilerParams(dimension_semantics=("arbitrary", "arbitrary")),
        cost_estimate=pl.CostEstimate(
            flops=4 * rows * chunks * chunk * width,
            transcendentals=rows * chunks * chunk,
            bytes_accessed=rows * width * 10 + (rows // block) * chunks * chunk * width * 2,
        ),
    )(*operands)


def shifted(value, axis, k):
    n = lax.axis_size(axis)
    return lax.ppermute(value, axis, [(i, (i + k) % n) for i in range(n)])

def body(
    tokens, shift_scale, branch_gate, final_gain, w_qkv, w_out, type_ids, head_w1, head_b1, head_w2
):
    inputs = tokens.astype(jnp.float32)
    modulated = (rms_normalize(inputs) * (1.0 + shift_scale[1]) + shift_scale[0]).astype(
        jnp.bfloat16
    )
    kinds = lax.axis_size("type")
    gathered = jnp.concatenate(
        [modulated] + [shifted(modulated, "type", k) for k in range(1, kinds)], axis=0
    )
    dim = w_qkv.shape[1]
    local_heads = w_qkv.shape[2] // HD
    parts = w_qkv.reshape(3, dim, local_heads, HD)
    scaled = (parts[0] * SCALE).astype(parts.dtype)
    arranged = jnp.stack([scaled, jnp.zeros_like(scaled), parts[1], parts[2]], axis=2)
    arranged = arranged.reshape(dim, local_heads, 4 * HD)
    arranged = jnp.roll(arranged, -lax.axis_index("x"), axis=1)
    projected = jnp.einsum(
        "rd,dje->jre", gathered, arranged, preferred_element_type=jnp.float32
    ).astype(jnp.bfloat16)
    mine = jnp.concatenate(
        [projected[0]] + [shifted(projected[k], "x", k) for k in range(1, local_heads)], axis=0
    )
    q_pad = mine[:, : 2 * HD]
    chunk = mine[:, 2 * HD :]
    z_n = lax.axis_size("z")
    zr = [(i, (i + 1) % z_n) for i in range(z_n)]
    zl = [(i, (i - 1) % z_n) for i in range(z_n)]
    yy = [(0, 1), (1, 0)]
    held = [chunk]
    state = None
    w_out_all = None
    for stage in range(4):
        if stage == 0:
            following = [
                lax.ppermute(chunk, "z", zr),
                lax.ppermute(chunk, "z", zl),
                lax.ppermute(chunk, "y", yy),
            ]
        elif stage == 1:
            pair = lax.ppermute(jnp.stack([held[0], held[2]]), "z", zr)
            following = [pair[0], pair[1], lax.ppermute(held[2], "z", zl)]
        elif stage == 2:
            following = [lax.ppermute(held[1], "z", zr)]
        else:
            following = []
        state = flash_step(q_pad, jnp.stack(held), state, stage == 0, stage == 3)
        if following:
            held, state = lax.optimization_barrier((following, state))
        if stage == 0:
            w_out_dep, held = lax.optimization_barrier((w_out, held))
            w_out_all = lax.all_gather(w_out_dep, "type", axis=0, tiled=True)
    attended = state[:, HD:]
    rows = tokens.shape[0]
    attended = attended.reshape(-1, rows, HD)
    owner = jnp.arange(local_heads * kinds)
    pick = ((lax.axis_index("x") - owner // kinds) % local_heads) * kinds + (
        lax.axis_index("type") - owner % kinds
    ) % kinds
    attended = jnp.take(attended, pick, axis=0)
    back = lax.all_to_all(attended, ("x", "type"), 0, 0, tiled=True)
    back = back.reshape(-1, kinds, rows, HD)
    back = jnp.transpose(back, (2, 1, 0, 3)).reshape(rows, -1)
    mixed = jnp.dot(back, w_out_all, preferred_element_type=jnp.float32)
    updated = (inputs + branch_gate * mixed).astype(jnp.bfloat16)
    final = (rms_normalize(updated.astype(jnp.float32)) * final_gain).astype(jnp.bfloat16)
    ids = jnp.broadcast_to(type_ids.astype(jnp.bfloat16), (rows, 128))
    ext = jnp.concatenate([final, ids], axis=1)
    joined = jnp.concatenate([ext] + [shifted(ext, "type", k) for k in range(1, kinds)], axis=0)
    final_all = joined[:, : final.shape[1]]
    kinds_all = joined[:, final.shape[1]].astype(jnp.int32)
    owned = head_w1.shape[0]
    first_kind = lax.axis_index("type") * owned
    result = jnp.zeros((final_all.shape[0], head_w2.shape[2]), jnp.float32)
    for which in range(owned):
        hidden = jnp.dot(final_all, head_w1[which], preferred_element_type=jnp.float32)
        hidden = jax.nn.gelu(hidden + head_b1[which].astype(jnp.float32)).astype(jnp.bfloat16)
        answer = jnp.dot(hidden, head_w2[which], preferred_element_type=jnp.float32)
        result = jnp.where((kinds_all == first_kind + which)[:, None], answer, result)
    result = result.reshape(kinds, rows, -1)
    head_out = result[0]
    for k in range(1, kinds):
        head_out = head_out + shifted(result[(-k) % kinds], "type", k)
    return (updated, head_out)


def solution(mesh):
    seq = mesh.shape["seq"]
    kinds = mesh.shape["type"]
    y_n = 2
    x_n = 4
    z_n = seq // (x_n * y_n)
    split = Mesh(mesh.devices.reshape(z_n, x_n, y_n, kinds), ("z", "x", "y", "type"))
    rows = P(("z", "x", "y", "type"), None)
    in_specs = (
        rows,
        P(),
        P(),
        P(),
        P(None, None, "type"),
        P("type", None),
        rows,
        P("type", None, None),
        P("type", None),
        P("type", None, None),
    )
    out_specs = (rows, rows)
    return jax.shard_map(body, mesh=split, in_specs=in_specs, out_specs=out_specs, check_vma=False)
```
